32 devices in a mesh: groups: 2 (over y), slide: 4 (over z), rep: 2 (over x), section: 2 (over core).
Axes of the slice: x: 2, y: 2, z: 4, core: 2. Of those that a mesh axis runs over, the one named last changes fastest.
Arguments:
- tile_features: bfloat16 [8, 12, 49, 1536], P(('groups', 'rep', 'section'), 'slide'), parts along dimension 0, may hold values from -6 to 6
- depth_weight: float32 [49, 1536], replicated, may hold values from -0.875 to 0.875
- depth_bias: float32 [1536], replicated, may hold values from -3 to 3
- norm_gain: float32 [1536], replicated, may hold values from 0.1 to 1.9
- norm_bias: float32 [1536], replicated, may hold values from -3 to 3
- up_weight: bfloat16 [1536, 3072], P(None, 'rep'), may hold values from -0.15625 to 0.15625
- up_bias: float32 [3072], P('rep'), may hold values from -3 to 3
- down_weight: bfloat16 [3072, 1536], P('rep'), may hold values from -0.109375 to 0.109375
- down_bias: float32 [1536], replicated, may hold values from -3 to 3
- layer_scale: float32 [1536], replicated, may hold values from 0.3 to 3
- head_gain: float32 [1536], replicated, may hold values from 0.1 to 1.9
- head_bias: float32 [1536], replicated, may hold values from -3 to 3
- embed_store: bfloat16 [8, 512, 1536], P(('groups', 'rep', 'section'), 'slide'), parts along dimension 0, may hold values from -6 to 6
- in_weight: bfloat16 [1536, 1024], P('slide'), may hold values from -0.15625 to 0.15625
- slide_gain: float32 [1024], replicated, may hold values from 0.1 to 1.9
- qkv_weight: bfloat16 [1024, 3072], P(None, 'slide'), may hold values from -0.1875 to 0.1875
- head_slopes: float32 [16], replicated, may hold values from 0.004 to 0.4
- tile_coords: int32 [8, 2, 512], P(('groups', 'rep', 'section')), parts along dimension 0, may hold values from 0 to 95, as said below
- valid_counts: int32 [8], P(('groups', 'rep', 'section')), parts along dimension 0, may hold values from 128 to 512, as said below
Outputs:
- fresh_embed: bfloat16 [8, 12, 1536], P(('groups', 'rep', 'section'), 'slide'), parts along dimension 0
- context: bfloat16 [8, 512, 1024], P(('groups', 'rep', 'section'), 'slide'), parts along dimension 0
The draws below stay inside these ranges and needn't reach their ends.
There are 2 independent parts, one for each index of `groups`. The reference program is written for one: setup_inputs(seed, part) draws one part's arguments, and reference() takes and returns one part's arrays. A program takes and returns all parts, laid end to end along the dimension named above; an argument that names none is the same for every part. Nothing has to cross between parts.
Inputs may be any that keep to these rules, and one draw needn't show every extreme that they name: `tile_coords`: each slide's 512 positions sit on distinct cells of a 96 by 96 grid, in raster order (by y, then x); the cells (0, 0) and (95, 95) are always among them. `valid_counts`: positions at or beyond a slide's count are padding.
All inputs are finite; a program needn't handle non-finite values.
Results may differ from the reference program's by a relative error of at most 0.0078.
Values may be sent and summed in bfloat16 or wider, within the bound.
No kernel may reach another device: no remote copies, remote signals or barrier semaphores. Data moves between devices by JAX's collectives and lax.ppermute only.
A program may use at most 64 MiB of HBM per device.

```python
import math
import jax
import jax.numpy as jnp
from jax import lax

C = 1536
HID = 3072
SIDE = 7
KER = 7
HEADS = 16
HDIM = 64
GRID = 96
TOK_DEV = 128
NEW_DEV = 3
DM = 1024
SLIDES = 4
SEQ = 512
NEW = 12
N_SLIDE = 4
N_REP = 2


def draw_tile_coords(key, part):
    cell_count = GRID * GRID

    def one_slide(slide_key):
        inner_cells = jax.random.permutation(slide_key, cell_count - 2) + 1
        chosen = jnp.concatenate([jnp.zeros((1,), jnp.int32), inner_cells[:SEQ - 2].astype(jnp.int32), jnp.full((1,), cell_count - 1, jnp.int32)])
        ordered = jnp.sort(chosen)
        return jnp.stack([ordered % GRID, ordered // GRID]).astype(jnp.int32)
    return jax.vmap(one_slide)(jax.random.split(jax.random.fold_in(key, 11), SLIDES))


def draw_valid_counts(key, part):
    base_key = jax.random.fold_in(key, 23)
    draw_key = jax.random.fold_in(base_key, 1)
    top_key = jax.random.fold_in(base_key, 2)
    low_key = jax.random.fold_in(base_key, 3)
    drawn = jax.random.randint(draw_key, (SLIDES,), SEQ // 4, SEQ + 1)
    top_slot = jax.random.randint(top_key, (), 0, SLIDES)
    low_slot = (top_slot + 1 + jax.random.randint(low_key, (), 0, SLIDES - 1)) % SLIDES
    slot_ids = jnp.arange(SLIDES)
    drawn = jnp.where(slot_ids == top_slot, SEQ, drawn)
    drawn = jnp.where(slot_ids == low_slot, SEQ // 4, drawn)
    return drawn.astype(jnp.int32)


def block_scale(own_key, shape, shards, smallest, top_value):
    def one(axis_at, blocks):
        heights = jax.random.uniform(jax.random.fold_in(jax.random.fold_in(own_key, 6), axis_at), (blocks,), jnp.float32, smallest / len(shards), top_value / len(shards))
        return jnp.repeat(jnp.exp(heights), shape[axis_at] // blocks).reshape((-1,) + (1,) * (len(shape) - axis_at - 1))

    level = one(*shards[0])
    for cut in shards[1:]:
        level = level * one(*cut)
    return level


def scatter_about(own_key, shape, deviation, most, cuts=(), kind=jnp.bfloat16):
    loudness = block_scale(own_key, shape, cuts, -0.22, 0.18) if cuts else 1.0
    array = jax.random.normal(own_key, shape, jnp.float32) * deviation * loudness
    return jnp.minimum(jnp.maximum(array, -most), most).astype(kind)


def setup_inputs(seed: int = 0, part: int = 0) -> dict:
    key_list = jax.random.split(jax.random.key(seed), 20)
    part_splits = jax.random.split(jax.random.fold_in(key_list[19], part), 20)
    tile_features = scatter_about(part_splits[0], (SLIDES, NEW, SIDE * SIDE, C), 1.0, 6.0, ((0, 4), (1, 4)))
    depth_weight = scatter_about(key_list[1], (KER * KER, C), (KER * KER) ** -0.5, 0.875, (), jnp.float32)
    depth_bias = scatter_about(key_list[2], (C,), 0.5, 3.0, (), jnp.float32)
    norm_gain = jnp.clip(1.0 + 0.18 * jax.random.normal(key_list[3], (C,), jnp.float32), 0.1, 1.9)
    norm_bias = scatter_about(key_list[4], (C,), 0.5, 3.0, (), jnp.float32)
    up_weight = scatter_about(key_list[5], (C, HID), C ** -0.5, 0.15625, ((1, 2),))
    up_bias = scatter_about(key_list[6], (HID,), 0.5, 3.0, ((0, 2),), jnp.float32)
    down_weight = scatter_about(key_list[7], (HID, C), HID ** -0.5, 0.109375, ((0, 2),))
    down_bias = scatter_about(key_list[8], (C,), 0.5, 3.0, (), jnp.float32)
    layer_scale = jnp.clip(jnp.exp(jax.random.uniform(key_list[9], (C,), jnp.float32, math.log(0.3), math.log(3.0))), 0.3, 3.0)
    head_gain = jnp.clip(1.0 + 0.18 * jax.random.normal(key_list[10], (C,), jnp.float32), 0.1, 1.9)
    head_bias = scatter_about(key_list[11], (C,), 0.5, 3.0, (), jnp.float32)
    embed_store = scatter_about(part_splits[12], (SLIDES, SEQ, C), 1.0, 6.0, ((0, 4), (1, 4)))
    in_weight = scatter_about(key_list[13], (C, DM), C ** -0.5, 0.15625, ((0, 4),))
    slide_gain = jnp.clip(1.0 + 0.18 * jax.random.normal(key_list[14], (DM,), jnp.float32), 0.1, 1.9)
    qkv_weight = scatter_about(key_list[15], (DM, 3 * DM), DM ** -0.5, 0.1875, ((1, 4),))
    head_slopes = jnp.clip(jnp.exp(jax.random.uniform(key_list[16], (HEADS,), jnp.float32, math.log(0.004), math.log(0.4))), 0.004, 0.4)
    tile_coords = draw_tile_coords(jax.random.fold_in(jax.random.fold_in(key_list[19], part), 71), part)
    valid_counts = draw_valid_counts(jax.random.fold_in(jax.random.fold_in(key_list[19], part), 71), part)
    return {"tile_features": tile_features, "depth_weight": depth_weight, "depth_bias": depth_bias, "norm_gain": norm_gain, "norm_bias": norm_bias, "up_weight": up_weight, "up_bias": up_bias, "down_weight": down_weight, "down_bias": down_bias, "layer_scale": layer_scale, "head_gain": head_gain, "head_bias": head_bias, "embed_store": embed_store, "in_weight": in_weight, "slide_gain": slide_gain, "qkv_weight": qkv_weight, "head_slopes": head_slopes, "tile_coords": tile_coords, "valid_counts": valid_counts}


def layer_norm(inputs, gain, shift, epsilon):
    center = lax.optimization_barrier(jnp.mean(inputs, axis=-1, keepdims=True))
    centered = inputs - center
    spread = lax.optimization_barrier(jnp.mean(centered * centered, axis=-1, keepdims=True))
    return centered * lax.rsqrt(spread + epsilon) * gain + shift

def depthwise(tile_data, depth_weight, depth_bias):
    tile_count = tile_data.shape[0]
    channels = tile_data.shape[-1]
    spatial = tile_data.reshape(tile_count, SIDE, SIDE, channels)
    margin = KER // 2
    padded = jnp.pad(spatial, ((0, 0), (margin, margin), (margin, margin), (0, 0)))
    running = jnp.zeros_like(spatial) + depth_bias
    for tap_row in range(KER):
        for tap_col in range(KER):
            running = running + padded[:, tap_row:tap_row + SIDE, tap_col:tap_col + SIDE, :] * depth_weight[tap_row * KER + tap_col]
    return running.reshape(tile_count, SIDE * SIDE, channels)

def unit_rms(values):
    return (values * lax.rsqrt(lax.optimization_barrier(jnp.mean(values * values, axis=-1, keepdims=True)) + 1e-06)).astype(jnp.bfloat16)

def reference(tile_features, depth_weight, depth_bias, norm_gain, norm_bias, up_weight, up_bias, down_weight, down_bias, layer_scale, head_gain, head_bias, embed_store, in_weight, slide_gain, qkv_weight, head_slopes, tile_coords, valid_counts):
    tile_data = tile_features.reshape(-1, SIDE * SIDE, C).astype(jnp.float32)
    convolved = depthwise(tile_data, depth_weight, depth_bias)
    normed = layer_norm(convolved, norm_gain, norm_bias, 1e-06).astype(jnp.bfloat16).reshape(-1, C)
    block_count = N_REP
    block_width = HID // block_count

    def add_block(running, block_index):
        offset = block_index * block_width
        up_cols = lax.dynamic_slice_in_dim(up_weight, offset, block_width, 1)
        bias_part = lax.dynamic_slice_in_dim(up_bias, offset, block_width, 0)
        hidden = jax.nn.gelu(jnp.dot(normed, up_cols, preferred_element_type=jnp.float32) + bias_part, approximate=False).astype(jnp.bfloat16)
        down_rows = lax.dynamic_slice_in_dim(down_weight, offset, block_width, 0)
        partial_sum = jnp.dot(hidden, down_rows, preferred_element_type=jnp.float32).astype(jnp.bfloat16)
        partial_sum = lax.optimization_barrier(partial_sum)
        return (running + partial_sum.astype(jnp.float32), None)
    summed, _ = lax.scan(add_block, jnp.zeros((normed.shape[0], C), jnp.float32), jnp.arange(block_count, dtype=jnp.int32))
    updated = tile_data + layer_scale * (summed.reshape(tile_data.shape) + down_bias)
    pooled = lax.optimization_barrier(jnp.mean(updated, axis=1))
    embedded = layer_norm(pooled, head_gain, head_bias, 1e-06).astype(jnp.bfloat16)
    fresh_embed = embedded.reshape(SLIDES, NEW, C)
    placed = embed_store.reshape(SLIDES, N_SLIDE, TOK_DEV, C)
    placed = placed.at[:, :, :NEW_DEV].set(fresh_embed.reshape(SLIDES, N_SLIDE, NEW_DEV, C))
    placed = placed.reshape(SLIDES, SEQ, C)
    inv_root = 1.0 / math.sqrt(HDIM)

    def slide_pass(packed):
        seq_rows, coord_pair, valid = packed
        projected = jnp.dot(seq_rows, in_weight, preferred_element_type=jnp.float32)
        normed_seq = layer_norm(projected, slide_gain, 0.0, 1e-05).astype(jnp.bfloat16)
        mixed = jnp.dot(normed_seq, qkv_weight, preferred_element_type=jnp.float32).reshape(SEQ, HEADS, 3, HDIM)
        unit_query = unit_rms(mixed[:, :, 0])
        unit_key = unit_rms(mixed[:, :, 1])
        value_rows = mixed[:, :, 2].astype(jnp.bfloat16)
        coord_x = coord_pair[0].astype(jnp.float32)
        coord_y = coord_pair[1].astype(jnp.float32)
        distance = jnp.abs(coord_x[:, None] - coord_x[None, :]) + jnp.abs(coord_y[:, None] - coord_y[None, :])
        positions = jnp.arange(SEQ, dtype=jnp.int32)
        key_ok = positions < valid

        def head_pass(head_pack):
            head_query, head_key, head_value, slope = head_pack
            scores = jnp.dot(head_query, head_key.T, preferred_element_type=jnp.float32) * inv_root - slope * distance
            weights = jnp.where(key_ok[None, :], jnp.exp(scores), 0.0).astype(jnp.bfloat16)
            totals = lax.optimization_barrier(jnp.sum(weights.astype(jnp.float32), axis=-1))
            weighted = jnp.dot(weights, head_value, preferred_element_type=jnp.float32)
            safe = jnp.where(key_ok, totals, 1.0)
            return jnp.where(key_ok[:, None], weighted / safe[:, None], 0.0).astype(jnp.bfloat16)
        heads_out = lax.map(head_pass, (unit_query.transpose(1, 0, 2), unit_key.transpose(1, 0, 2), value_rows.transpose(1, 0, 2), head_slopes))
        return heads_out.transpose(1, 0, 2).reshape(SEQ, HEADS * HDIM)
    context = lax.map(slide_pass, (placed, tile_coords, valid_counts))
    return (fresh_embed, context)
```

```python
import math

import jax
import jax.numpy as jnp
from jax import lax
from jax.sharding import PartitionSpec as P

SIDE = 7
KER = 7
HDIM = 64


def layer_norm(inputs, gain, shift, epsilon):
    center = jnp.mean(inputs, axis=-1, keepdims=True)
    centered = inputs - center
    spread = jnp.mean(centered * centered, axis=-1, keepdims=True)
    return centered * lax.rsqrt(spread + epsilon) * gain + shift


def depthwise(tile_data, depth_weight, depth_bias):
    tile_count = tile_data.shape[0]
    channels = tile_data.shape[-1]
    spatial = tile_data.reshape(tile_count, SIDE, SIDE, channels)
    margin = KER // 2
    padded = jnp.pad(spatial, ((0, 0), (margin, margin), (margin, margin), (0, 0)))
    running = jnp.zeros_like(spatial) + depth_bias
    for tap_row in range(KER):
        for tap_col in range(KER):
            running = (
                running
                + padded[:, tap_row : tap_row + SIDE, tap_col : tap_col + SIDE, :]
                * depth_weight[tap_row * KER + tap_col]
            )
    return running.reshape(tile_count, SIDE * SIDE, channels)


def normalize_heads(values):
    lead = values.shape[:-1]
    grouped = values.reshape(lead + (-1, 3, HDIM))
    paired = grouped[..., :2, :]
    scaled = paired * lax.rsqrt(jnp.mean(paired * paired, axis=-1, keepdims=True) + 1e-06)
    joined = jnp.concatenate([scaled, grouped[..., 2:, :]], axis=-2)
    return joined.astype(jnp.bfloat16).reshape(lead + (-1,))


def project(rows, weight_parts, slide_gain):
    projected = jnp.einsum(
        "nk,skc->nsc", rows, weight_parts, preferred_element_type=jnp.float32
    ).reshape(rows.shape[0], -1)
    return layer_norm(projected, slide_gain, 0.0, 1e-05).astype(jnp.bfloat16)


def on_device(
    tile_features,
    depth_weight,
    depth_bias,
    norm_gain,
    norm_bias,
    up_weight,
    up_bias,
    down_weight,
    down_bias,
    layer_scale,
    head_gain,
    head_bias,
    embed_store,
    in_weight,
    slide_gain,
    qkv_weight,
    head_slopes,
    tile_coords,
    valid_counts,
):
    n_sec = lax.axis_size("section")
    col_part = in_weight.shape[1] // n_sec
    my_cols = lax.dynamic_slice_in_dim(
        in_weight, lax.axis_index("section") * col_part, col_part, 1
    )
    cols_full = lax.all_gather(my_cols, "slide", axis=0, tiled=True)
    weight_parts = lax.all_gather(cols_full, "section", axis=0, tiled=False)

    fresh_count = tile_features.shape[1]
    stale_normed = project(embed_store[0], weight_parts, slide_gain)
    stale_all = lax.all_gather(stale_normed, "slide", axis=0, tiled=False)
    stale_mixed = normalize_heads(
        jnp.einsum("rnk,kc->rnc", stale_all, qkv_weight, preferred_element_type=jnp.float32)
    )

    tile_data = tile_features[0].astype(jnp.float32)
    channels = tile_data.shape[-1]
    convolved = depthwise(tile_data, depth_weight, depth_bias)
    normed = (
        layer_norm(convolved, norm_gain, norm_bias, 1e-06)
        .astype(jnp.bfloat16)
        .reshape(-1, channels)
    )
    hidden = jax.nn.gelu(
        jnp.dot(
            lax.all_gather(normed, "rep", axis=0, tiled=True),
            up_weight,
            preferred_element_type=jnp.float32,
        )
        + up_bias,
        approximate=False,
    ).astype(jnp.bfloat16)
    summed = lax.psum_scatter(
        jnp.dot(hidden, down_weight, preferred_element_type=jnp.float32).astype(jnp.bfloat16),
        "rep",
        scatter_dimension=0,
        tiled=True,
    ).astype(jnp.float32)
    updated = tile_data + layer_scale * (summed.reshape(tile_data.shape) + down_bias)
    pooled = jnp.mean(updated, axis=1)
    embedded = layer_norm(pooled, head_gain, head_bias, 1e-06).astype(jnp.bfloat16)

    fresh_normed = project(embedded, weight_parts, slide_gain)
    fresh_all = lax.all_gather(fresh_normed, "slide", axis=0, tiled=False)
    fresh_mixed = normalize_heads(
        jnp.einsum("rnk,kc->rnc", fresh_all, qkv_weight, preferred_element_type=jnp.float32)
    )
    local_heads = jnp.concatenate([fresh_mixed, stale_mixed[:, fresh_count:]], axis=1)
    n_slide = local_heads.shape[0]
    seq_len = n_slide * local_heads.shape[1]
    local_heads = local_heads.reshape(seq_len, -1)

    heads_here = local_heads.shape[1] // (3 * HDIM)
    arranged = local_heads.reshape(seq_len, heads_here, 3, HDIM)
    queries = arranged[:, :, 0]
    key_rows = arranged[:, :, 1]
    value_rows = arranged[:, :, 2]
    my_slopes = lax.dynamic_slice_in_dim(
        head_slopes, lax.axis_index("slide") * heads_here, heads_here, 0
    )
    coord_x = tile_coords[0, 0].astype(jnp.float32)
    coord_y = tile_coords[0, 1].astype(jnp.float32)
    valid = valid_counts[0]
    key_ok = jnp.arange(seq_len, dtype=jnp.int32) < valid
    inv_root = 1.0 / math.sqrt(HDIM)

    distance = jnp.abs(coord_x[:, None] - coord_x[None, :]) + jnp.abs(
        coord_y[:, None] - coord_y[None, :]
    )
    scores = (
        jnp.einsum("qhd,khd->hqk", queries, key_rows, preferred_element_type=jnp.float32)
        * inv_root
        - my_slopes[:, None, None] * distance[None]
    )
    weights = jnp.where(key_ok[None, None, :], jnp.exp(scores), 0.0).astype(jnp.bfloat16)
    totals = jnp.sum(weights, axis=-1, dtype=jnp.float32)
    weighted = jnp.einsum("hqk,khd->qhd", weights, value_rows, preferred_element_type=jnp.float32)
    safe = jnp.where(key_ok[None, :], totals, 1.0)
    attended = jnp.where(key_ok[:, None, None], weighted / safe.T[:, :, None], 0.0)
    attended = attended.astype(jnp.bfloat16).reshape(seq_len, heads_here * HDIM)
    context = lax.all_to_all(attended, "slide", split_axis=0, concat_axis=1, tiled=True)
    return (embedded[None], context[None])


def solution(mesh):
    in_specs = (
        P(("groups", "rep", "section"), "slide", None, None),
        P(),
        P(),
        P(),
        P(),
        P(None, "rep"),
        P("rep"),
        P("rep", None),
        P(),
        P(),
        P(),
        P(),
        P(("groups", "rep", "section"), "slide", None),
        P("slide", None),
        P(),
        P(None, "slide"),
        P(),
        P(("groups", "rep", "section"), None, None),
        P(("groups", "rep", "section")),
    )
    out_specs = (
        P(("groups", "rep", "section"), "slide", None),
        P(("groups", "rep", "section"), "slide", None),
    )
    return jax.shard_map(
        on_device, mesh=mesh, in_specs=in_specs, out_specs=out_specs, check_vma=False
    )
```

```python
import math

import jax
import jax.numpy as jnp
from jax import lax
from jax.experimental import pallas as pl
from jax.experimental.pallas import tpu as pltpu
from jax.sharding import PartitionSpec as P

SIDE = 7
KER = 7
HDIM = 64
LANES = 128


def layer_norm(inputs, gain, shift, epsilon):
    center = jnp.mean(inputs, axis=-1, keepdims=True)
    centered = inputs - center
    spread = jnp.mean(centered * centered, axis=-1, keepdims=True)
    return centered * lax.rsqrt(spread + epsilon) * gain + shift


def dw_ln_kernel(x_ref, w_ref, b_ref, g_ref, nb_ref, o_ref, conv_ref):
    C = x_ref.shape[-1]
    jrow = lax.broadcasted_iota(jnp.int32, (8, LANES), 0)
    masks = [((jrow + (bb - 3)) >= 0) & ((jrow + (bb - 3)) < SIDE) for bb in range(KER)]
    def chunk(ci, carry):
        c0 = pl.multiple_of(ci * LANES, LANES)
        rows = [x_ref[0, i, :, pl.ds(c0, LANES)].astype(jnp.float32) for i in range(SIDE)]
        bias = jnp.broadcast_to(b_ref[:, pl.ds(c0, LANES)], (8, LANES))
        acc = [bias for _ in range(SIDE)]
        for ip in range(SIDE):
            for bb in range(KER):
                s = bb - 3
                sh = rows[ip] if s == 0 else pltpu.roll(rows[ip], shift=(-s) % 8, axis=0)
                sh = jnp.where(masks[bb], sh, 0.0)
                for a in range(KER):
                    i = ip - (a - 3)
                    if 0 <= i < SIDE:
                        wv = jnp.broadcast_to(w_ref[pl.ds(a * KER + bb, 1), pl.ds(c0, LANES)], (8, LANES))
                        acc[i] = acc[i] + sh * wv
        for i in range(SIDE):
            conv_ref[i, :, pl.ds(c0, LANES)] = acc[i]
        return carry
    lax.fori_loop(0, C // LANES, chunk, 0)
    g = g_ref[...]
    nb = nb_ref[...]
    for i in range(SIDE):
        v = conv_ref[i]
        mean = jnp.mean(v, axis=-1, keepdims=True)
        cen = v - mean
        var = jnp.mean(cen * cen, axis=-1, keepdims=True)
        o_ref[0, i] = (cen * lax.rsqrt(var + 1e-06) * g + nb).astype(o_ref.dtype)

def dw_ln(tiles, depth_weight, depth_bias, norm_gain, norm_bias):
    T, _, C = tiles.shape
    x = jnp.pad(tiles.reshape(T, SIDE, SIDE, C), ((0, 0), (0, 0), (0, 1), (0, 0)))
    out = pl.pallas_call(
        dw_ln_kernel,
        grid=(T,),
        in_specs=[
            pl.BlockSpec((1, SIDE, 8, C), lambda t: (t, 0, 0, 0)),
            pl.BlockSpec((KER * KER, C), lambda t: (0, 0)),
            pl.BlockSpec((1, C), lambda t: (0, 0)),
            pl.BlockSpec((1, C), lambda t: (0, 0)),
            pl.BlockSpec((1, C), lambda t: (0, 0)),
        ],
        out_specs=pl.BlockSpec((1, SIDE, 8, C), lambda t: (t, 0, 0, 0)),
        out_shape=jax.ShapeDtypeStruct((T, SIDE, 8, C), jnp.bfloat16),
        scratch_shapes=[pltpu.VMEM((SIDE, 8, C), jnp.float32)],
    )(x, depth_weight, depth_bias[None], norm_gain[None], norm_bias[None])
    return out[:, :, :SIDE].reshape(T * SIDE * SIDE, C)


def normalize_heads(values):
    lead = values.shape[:-1]
    grouped = values.reshape(lead + (-1, 3, HDIM))
    paired = grouped[..., :2, :]
    scaled = paired * lax.rsqrt(jnp.mean(paired * paired, axis=-1, keepdims=True) + 1e-06)
    joined = jnp.concatenate([scaled, grouped[..., 2:, :]], axis=-2)
    return joined.astype(jnp.bfloat16).reshape(lead + (-1,))


def project(rows, weight_parts, slide_gain):
    projected = jnp.einsum(
        "nk,skc->nsc", rows, weight_parts, preferred_element_type=jnp.float32
    ).reshape(rows.shape[0], -1)
    return layer_norm(projected, slide_gain, 0.0, 1e-05).astype(jnp.bfloat16)


def on_device(
    tile_features,
    depth_weight,
    depth_bias,
    norm_gain,
    norm_bias,
    up_weight,
    up_bias,
    down_weight,
    down_bias,
    layer_scale,
    head_gain,
    head_bias,
    embed_store,
    in_weight,
    slide_gain,
    qkv_weight,
    head_slopes,
    tile_coords,
    valid_counts,
):
    n_sec = lax.axis_size("section")
    col_part = in_weight.shape[1] // n_sec
    my_cols = lax.dynamic_slice_in_dim(
        in_weight, lax.axis_index("section") * col_part, col_part, 1
    )
    cols_full = lax.all_gather(my_cols, "slide", axis=0, tiled=True)
    weight_parts = lax.all_gather(cols_full, "section", axis=0, tiled=False)

    fresh_count = tile_features.shape[1]
    stale_normed = project(embed_store[0], weight_parts, slide_gain)
    stale_all = lax.all_gather(stale_normed, "slide", axis=0, tiled=False)
    stale_mixed = normalize_heads(
        jnp.einsum("rnk,kc->rnc", stale_all, qkv_weight, preferred_element_type=jnp.float32)
    )

    tile_data = tile_features[0].astype(jnp.float32)
    normed = dw_ln(tile_features[0], depth_weight, depth_bias, norm_gain, norm_bias)
    hidden = jax.nn.gelu(
        jnp.dot(
            lax.all_gather(normed, "rep", axis=0, tiled=True),
            up_weight,
            preferred_element_type=jnp.float32,
        )
        + up_bias,
        approximate=False,
    ).astype(jnp.bfloat16)
    summed = lax.psum_scatter(
        jnp.dot(hidden, down_weight, preferred_element_type=jnp.float32).astype(jnp.bfloat16),
        "rep",
        scatter_dimension=0,
        tiled=True,
    ).astype(jnp.float32)
    updated = tile_data + layer_scale * (summed.reshape(tile_data.shape) + down_bias)
    pooled = jnp.mean(updated, axis=1)
    embedded = layer_norm(pooled, head_gain, head_bias, 1e-06).astype(jnp.bfloat16)

    fresh_normed = project(embedded, weight_parts, slide_gain)
    fresh_all = lax.all_gather(fresh_normed, "slide", axis=0, tiled=False)
    fresh_mixed = normalize_heads(
        jnp.einsum("rnk,kc->rnc", fresh_all, qkv_weight, preferred_element_type=jnp.float32)
    )
    local_heads = jnp.concatenate([fresh_mixed, stale_mixed[:, fresh_count:]], axis=1)
    n_slide = local_heads.shape[0]
    seq_len = n_slide * local_heads.shape[1]
    local_heads = local_heads.reshape(seq_len, -1)

    heads_here = local_heads.shape[1] // (3 * HDIM)
    arranged = local_heads.reshape(seq_len, heads_here, 3, HDIM)
    queries = arranged[:, :, 0]
    key_rows = arranged[:, :, 1]
    value_rows = arranged[:, :, 2]
    my_slopes = lax.dynamic_slice_in_dim(
        head_slopes, lax.axis_index("slide") * heads_here, heads_here, 0
    )
    coord_x = tile_coords[0, 0].astype(jnp.float32)
    coord_y = tile_coords[0, 1].astype(jnp.float32)
    valid = valid_counts[0]
    key_ok = jnp.arange(seq_len, dtype=jnp.int32) < valid
    inv_root = 1.0 / math.sqrt(HDIM)

    distance = jnp.abs(coord_x[:, None] - coord_x[None, :]) + jnp.abs(
        coord_y[:, None] - coord_y[None, :]
    )
    scores = (
        jnp.einsum("qhd,khd->hqk", queries, key_rows, preferred_element_type=jnp.float32)
        * inv_root
        - my_slopes[:, None, None] * distance[None]
    )
    weights = jnp.where(key_ok[None, None, :], jnp.exp(scores), 0.0).astype(jnp.bfloat16)
    totals = jnp.sum(weights, axis=-1, dtype=jnp.float32)
    weighted = jnp.einsum("hqk,khd->qhd", weights, value_rows, preferred_element_type=jnp.float32)
    safe = jnp.where(key_ok[None, :], totals, 1.0)
    attended = jnp.where(key_ok[:, None, None], weighted / safe.T[:, :, None], 0.0)
    attended = attended.astype(jnp.bfloat16).reshape(seq_len, heads_here * HDIM)
    context = lax.all_to_all(attended, "slide", split_axis=0, concat_axis=1, tiled=True)
    return (embedded[None], context[None])


def solution(mesh):
    in_specs = (
        P(("groups", "rep", "section"), "slide", None, None),
        P(),
        P(),
        P(),
        P(),
        P(None, "rep"),
        P("rep"),
        P("rep", None),
        P(),
        P(),
        P(),
        P(),
        P(("groups", "rep", "section"), "slide", None),
        P("slide", None),
        P(),
        P(None, "slide"),
        P(),
        P(("groups", "rep", "section"), None, None),
        P(("groups", "rep", "section")),
    )
    out_specs = (
        P(("groups", "rep", "section"), "slide", None),
        P(("groups", "rep", "section"), "slide", None),
    )
    return jax.shard_map(
        on_device, mesh=mesh, in_specs=in_specs, out_specs=out_specs, check_vma=False
    )
```

```python
import math

import jax
import jax.numpy as jnp
from jax import lax
from jax.experimental import pallas as pl
from jax.experimental.pallas import tpu as pltpu
from jax.sharding import PartitionSpec as P

SIDE = 7
KER = 7
HDIM = 64
LANES = 128


def layer_norm(inputs, gain, shift, epsilon):
    center = jnp.mean(inputs, axis=-1, keepdims=True)
    centered = inputs - center
    spread = jnp.mean(centered * centered, axis=-1, keepdims=True)
    return centered * lax.rsqrt(spread + epsilon) * gain + shift


def dw_ln_kernel(x_ref, w_ref, b_ref, g_ref, nb_ref, o_ref, conv_ref):
    C = x_ref.shape[-1]
    jrow = lax.broadcasted_iota(jnp.int32, (8, LANES), 0)
    masks = [((jrow + (bb - 3)) >= 0) & ((jrow + (bb - 3)) < SIDE) for bb in range(KER)]
    def chunk(ci, carry):
        c0 = pl.multiple_of(ci * LANES, LANES)
        rows = [x_ref[0, i, :, pl.ds(c0, LANES)].astype(jnp.float32) for i in range(SIDE)]
        bias = jnp.broadcast_to(b_ref[:, pl.ds(c0, LANES)], (8, LANES))
        acc = [bias for _ in range(SIDE)]
        for ip in range(SIDE):
            for bb in range(KER):
                s = bb - 3
                sh = rows[ip] if s == 0 else pltpu.roll(rows[ip], shift=(-s) % 8, axis=0)
                sh = jnp.where(masks[bb], sh, 0.0)
                for a in range(KER):
                    i = ip - (a - 3)
                    if 0 <= i < SIDE:
                        wv = jnp.broadcast_to(w_ref[pl.ds(a * KER + bb, 1), pl.ds(c0, LANES)], (8, LANES))
                        acc[i] = acc[i] + sh * wv
        for i in range(SIDE):
            conv_ref[i, :, pl.ds(c0, LANES)] = acc[i]
        return carry
    lax.fori_loop(0, C // LANES, chunk, 0)
    g = g_ref[...]
    nb = nb_ref[...]
    for i in range(SIDE):
        v = conv_ref[i]
        mean = jnp.mean(v, axis=-1, keepdims=True)
        cen = v - mean
        var = jnp.mean(cen * cen, axis=-1, keepdims=True)
        o_ref[0, i] = (cen * lax.rsqrt(var + 1e-06) * g + nb).astype(o_ref.dtype)

def dw_ln(tiles, depth_weight, depth_bias, norm_gain, norm_bias):
    T, _, C = tiles.shape
    x = jnp.pad(tiles.reshape(T, SIDE, SIDE, C), ((0, 0), (0, 0), (0, 1), (0, 0)))
    out = pl.pallas_call(
        dw_ln_kernel,
        grid=(T,),
        in_specs=[
            pl.BlockSpec((1, SIDE, 8, C), lambda t: (t, 0, 0, 0)),
            pl.BlockSpec((KER * KER, C), lambda t: (0, 0)),
            pl.BlockSpec((1, C), lambda t: (0, 0)),
            pl.BlockSpec((1, C), lambda t: (0, 0)),
            pl.BlockSpec((1, C), lambda t: (0, 0)),
        ],
        out_specs=pl.BlockSpec((1, SIDE, 8, C), lambda t: (t, 0, 0, 0)),
        out_shape=jax.ShapeDtypeStruct((T, SIDE, 8, C), jnp.bfloat16),
        scratch_shapes=[pltpu.VMEM((SIDE, 8, C), jnp.float32)],
    )(x, depth_weight, depth_bias[None], norm_gain[None], norm_bias[None])
    return out[:, :, :SIDE].reshape(T * SIDE * SIDE, C)


def normalize_heads(values):
    lead = values.shape[:-1]
    grouped = values.reshape(lead + (-1, 3, HDIM))
    paired = grouped[..., :2, :]
    scaled = paired * lax.rsqrt(jnp.mean(paired * paired, axis=-1, keepdims=True) + 1e-06)
    joined = jnp.concatenate([scaled, grouped[..., 2:, :]], axis=-2)
    return joined.astype(jnp.bfloat16).reshape(lead + (-1,))


def project(rows, weight_parts, slide_gain):
    projected = jnp.einsum(
        "nk,skc->nsc", rows, weight_parts, preferred_element_type=jnp.float32
    ).reshape(rows.shape[0], -1)
    return layer_norm(projected, slide_gain, 0.0, 1e-05).astype(jnp.bfloat16)


def on_device(
    tile_features,
    depth_weight,
    depth_bias,
    norm_gain,
    norm_bias,
    up_weight,
    up_bias,
    down_weight,
    down_bias,
    layer_scale,
    head_gain,
    head_bias,
    embed_store,
    in_weight,
    slide_gain,
    qkv_weight,
    head_slopes,
    tile_coords,
    valid_counts,
):
    n_sec = lax.axis_size("section")
    col_part = in_weight.shape[1] // n_sec
    my_cols = lax.dynamic_slice_in_dim(
        in_weight, lax.axis_index("section") * col_part, col_part, 1
    )
    cols_full = lax.all_gather(my_cols, "slide", axis=0, tiled=True)
    weight_parts = lax.all_gather(cols_full, "section", axis=0, tiled=False)

    fresh_count = tile_features.shape[1]
    stale_normed = project(embed_store[0], weight_parts, slide_gain)
    stale_all = lax.all_gather(stale_normed, "slide", axis=0, tiled=False)
    stale_mixed = normalize_heads(
        jnp.einsum("rnk,kc->rnc", stale_all, qkv_weight, preferred_element_type=jnp.float32)
    )

    tile_data = tile_features[0].astype(jnp.float32)
    fresh_count = tile_data.shape[0]
    n_rep = lax.axis_size("rep")
    my_rep = lax.axis_index("rep")
    n_slide = lax.axis_size("slide")
    my_slide = lax.axis_index("slide")
    normed = dw_ln(tile_features[0], depth_weight, depth_bias, norm_gain, norm_bias)

    def block_sums(rows):
        hidden = jax.nn.gelu(
            jnp.dot(rows, up_weight, preferred_element_type=jnp.float32) + up_bias,
            approximate=False,
        ).astype(jnp.bfloat16)
        part = jnp.dot(hidden, down_weight, preferred_element_type=jnp.float32).astype(
            jnp.bfloat16
        )
        return jnp.sum(part.astype(jnp.float32).reshape(tile_data.shape), axis=1)

    received = [
        lax.ppermute(normed, "rep", perm=[(r, (r + k) % n_rep) for r in range(n_rep)])
        for k in range(1, n_rep)
    ]
    positions = tile_data.shape[1]
    own_term = jnp.mean(tile_data, axis=1) + layer_scale * (
        block_sums(normed) / positions + down_bias
    )
    slots = jnp.zeros((n_rep, n_slide) + own_term.shape, jnp.float32)
    slots = lax.dynamic_update_slice(slots, own_term[None, None], (my_rep, my_slide, 0, 0))
    for k, rows in enumerate(received, start=1):
        term = layer_scale * (block_sums(rows) / positions)
        slots = lax.dynamic_update_slice(
            slots, term[None, None], ((my_rep - k) % n_rep, my_slide, 0, 0)
        )
    pooled_all = lax.psum(slots, ("slide", "rep"))
    pooled = lax.dynamic_index_in_dim(pooled_all, my_rep, 0, keepdims=False)
    pooled = pooled.reshape(n_slide * fresh_count, -1)
    embedded_all = layer_norm(pooled, head_gain, head_bias, 1e-06).astype(jnp.bfloat16)
    embedded = lax.dynamic_slice_in_dim(embedded_all, my_slide * fresh_count, fresh_count, 0)

    fresh_normed = project(embedded_all, weight_parts, slide_gain)
    fresh_mixed = normalize_heads(
        jnp.dot(fresh_normed, qkv_weight, preferred_element_type=jnp.float32)
    ).reshape(n_slide, fresh_count, -1)
    local_heads = jnp.concatenate([fresh_mixed, stale_mixed[:, fresh_count:]], axis=1)
    n_slide = local_heads.shape[0]
    seq_len = n_slide * local_heads.shape[1]
    local_heads = local_heads.reshape(seq_len, -1)

    heads_here = local_heads.shape[1] // (3 * HDIM)
    arranged = local_heads.reshape(seq_len, heads_here, 3, HDIM)
    queries = arranged[:, :, 0]
    key_rows = arranged[:, :, 1]
    value_rows = arranged[:, :, 2]
    my_slopes = lax.dynamic_slice_in_dim(
        head_slopes, lax.axis_index("slide") * heads_here, heads_here, 0
    )
    coord_x = tile_coords[0, 0].astype(jnp.float32)
    coord_y = tile_coords[0, 1].astype(jnp.float32)
    valid = valid_counts[0]
    key_ok = jnp.arange(seq_len, dtype=jnp.int32) < valid
    inv_root = 1.0 / math.sqrt(HDIM)

    distance = jnp.abs(coord_x[:, None] - coord_x[None, :]) + jnp.abs(
        coord_y[:, None] - coord_y[None, :]
    )
    scores = (
        jnp.einsum("qhd,khd->hqk", queries, key_rows, preferred_element_type=jnp.float32)
        * inv_root
        - my_slopes[:, None, None] * distance[None]
    )
    weights = jnp.where(key_ok[None, None, :], jnp.exp(scores), 0.0).astype(jnp.bfloat16)
    totals = jnp.sum(weights, axis=-1, dtype=jnp.float32)
    weighted = jnp.einsum("hqk,khd->qhd", weights, value_rows, preferred_element_type=jnp.float32)
    safe = jnp.where(key_ok[None, :], totals, 1.0)
    attended = jnp.where(key_ok[:, None, None], weighted / safe.T[:, :, None], 0.0)
    attended = attended.astype(jnp.bfloat16).reshape(seq_len, heads_here * HDIM)
    context = lax.all_to_all(attended, "slide", split_axis=0, concat_axis=1, tiled=True)
    return (embedded[None], context[None])


def solution(mesh):
    in_specs = (
        P(("groups", "rep", "section"), "slide", None, None),
        P(),
        P(),
        P(),
        P(),
        P(None, "rep"),
        P("rep"),
        P("rep", None),
        P(),
        P(),
        P(),
        P(),
        P(("groups", "rep", "section"), "slide", None),
        P("slide", None),
        P(),
        P(None, "slide"),
        P(),
        P(("groups", "rep", "section"), None, None),
        P(("groups", "rep", "section")),
    )
    out_specs = (
        P(("groups", "rep", "section"), "slide", None),
        P(("groups", "rep", "section"), "slide", None),
    )
    return jax.shard_map(
        on_device, mesh=mesh, in_specs=in_specs, out_specs=out_specs, check_vma=False
    )
```

```python
import math

import jax
import jax.numpy as jnp
from jax import lax
from jax.experimental import pallas as pl
from jax.experimental.pallas import tpu as pltpu
from jax.sharding import PartitionSpec as P

SIDE = 7
KER = 7
HDIM = 64
LANES = 128


def layer_norm(inputs, gain, shift, epsilon):
    center = jnp.mean(inputs, axis=-1, keepdims=True)
    centered = inputs - center
    spread = jnp.mean(centered * centered, axis=-1, keepdims=True)
    return centered * lax.rsqrt(spread + epsilon) * gain + shift


def dw_ln_kernel(x_ref, w_ref, b_ref, g_ref, nb_ref, o_ref, conv_ref):
    C = x_ref.shape[-1]
    jrow = lax.broadcasted_iota(jnp.int32, (8, LANES), 0)
    masks = [((jrow + (bb - 3)) >= 0) & ((jrow + (bb - 3)) < SIDE) for bb in range(KER)]
    def chunk(ci, carry):
        c0 = pl.multiple_of(ci * LANES, LANES)
        rows = [x_ref[0, i, :, pl.ds(c0, LANES)].astype(jnp.float32) for i in range(SIDE)]
        bias = jnp.broadcast_to(b_ref[:, pl.ds(c0, LANES)], (8, LANES))
        acc = [bias for _ in range(SIDE)]
        for ip in range(SIDE):
            for bb in range(KER):
                s = bb - 3
                sh = rows[ip] if s == 0 else pltpu.roll(rows[ip], shift=(-s) % 8, axis=0)
                sh = jnp.where(masks[bb], sh, 0.0)
                for a in range(KER):
                    i = ip - (a - 3)
                    if 0 <= i < SIDE:
                        wv = jnp.broadcast_to(w_ref[pl.ds(a * KER + bb, 1), pl.ds(c0, LANES)], (8, LANES))
                        acc[i] = acc[i] + sh * wv
        for i in range(SIDE):
            conv_ref[i, :, pl.ds(c0, LANES)] = acc[i]
        return carry
    lax.fori_loop(0, C // LANES, chunk, 0)
    g = g_ref[...]
    nb = nb_ref[...]
    for i in range(SIDE):
        v = conv_ref[i]
        mean = jnp.mean(v, axis=-1, keepdims=True)
        cen = v - mean
        var = jnp.mean(cen * cen, axis=-1, keepdims=True)
        o_ref[0, i] = (cen * lax.rsqrt(var + 1e-06) * g + nb).astype(o_ref.dtype)

def dw_ln(tiles, depth_weight, depth_bias, norm_gain, norm_bias):
    T, _, C = tiles.shape
    x = jnp.pad(tiles.reshape(T, SIDE, SIDE, C), ((0, 0), (0, 0), (0, 1), (0, 0)))
    out = pl.pallas_call(
        dw_ln_kernel,
        grid=(T,),
        in_specs=[
            pl.BlockSpec((1, SIDE, 8, C), lambda t: (t, 0, 0, 0)),
            pl.BlockSpec((KER * KER, C), lambda t: (0, 0)),
            pl.BlockSpec((1, C), lambda t: (0, 0)),
            pl.BlockSpec((1, C), lambda t: (0, 0)),
            pl.BlockSpec((1, C), lambda t: (0, 0)),
        ],
        out_specs=pl.BlockSpec((1, SIDE, 8, C), lambda t: (t, 0, 0, 0)),
        out_shape=jax.ShapeDtypeStruct((T, SIDE, 8, C), jnp.bfloat16),
        scratch_shapes=[pltpu.VMEM((SIDE, 8, C), jnp.float32)],
    )(x, depth_weight, depth_bias[None], norm_gain[None], norm_bias[None])
    return out[:, :, :SIDE].reshape(T * SIDE * SIDE, C)


def normalize_heads(values):
    lead = values.shape[:-1]
    grouped = values.reshape(lead + (-1, 3, HDIM))
    paired = grouped[..., :2, :]
    scaled = paired * lax.rsqrt(jnp.mean(paired * paired, axis=-1, keepdims=True) + 1e-06)
    joined = jnp.concatenate([scaled, grouped[..., 2:, :]], axis=-2)
    return joined.astype(jnp.bfloat16).reshape(lead + (-1,))


def project(rows, weight_parts, slide_gain):
    projected = jnp.einsum(
        "nk,skc->nsc", rows, weight_parts, preferred_element_type=jnp.float32
    ).reshape(rows.shape[0], -1)
    return layer_norm(projected, slide_gain, 0.0, 1e-05).astype(jnp.bfloat16)


def on_device(
    tile_features,
    depth_weight,
    depth_bias,
    norm_gain,
    norm_bias,
    up_weight,
    up_bias,
    down_weight,
    down_bias,
    layer_scale,
    head_gain,
    head_bias,
    embed_store,
    in_weight,
    slide_gain,
    qkv_weight,
    head_slopes,
    tile_coords,
    valid_counts,
):
    n_sec = lax.axis_size("section")
    col_part = in_weight.shape[1] // n_sec
    my_cols = lax.dynamic_slice_in_dim(
        in_weight, lax.axis_index("section") * col_part, col_part, 1
    )
    cols_full = lax.all_gather(my_cols, "slide", axis=0, tiled=True)
    weight_parts = lax.all_gather(cols_full, "section", axis=0, tiled=False)

    fresh_count = tile_features.shape[1]
    stale_normed = project(embed_store[0], weight_parts, slide_gain)
    stale_all = lax.all_gather(stale_normed, "slide", axis=0, tiled=False)
    stale_mixed = normalize_heads(
        jnp.einsum("rnk,kc->rnc", stale_all, qkv_weight, preferred_element_type=jnp.float32)
    )

    tile_data = tile_features[0].astype(jnp.float32)
    fresh_count = tile_data.shape[0]
    n_rep = lax.axis_size("rep")
    my_rep = lax.axis_index("rep")
    n_slide = lax.axis_size("slide")
    my_slide = lax.axis_index("slide")
    normed = dw_ln(tile_features[0], depth_weight, depth_bias, norm_gain, norm_bias)

    def block_sums(rows):
        hidden = jax.nn.gelu(
            jnp.dot(rows, up_weight, preferred_element_type=jnp.float32) + up_bias,
            approximate=False,
        ).astype(jnp.bfloat16)
        part = jnp.dot(hidden, down_weight, preferred_element_type=jnp.float32).astype(
            jnp.bfloat16
        )
        return jnp.sum(part.astype(jnp.float32).reshape(tile_data.shape), axis=1)

    received = [
        lax.ppermute(normed, "rep", perm=[(r, (r + k) % n_rep) for r in range(n_rep)])
        for k in range(1, n_rep)
    ]
    positions = tile_data.shape[1]
    own_term = jnp.mean(tile_data, axis=1) + layer_scale * (
        block_sums(normed) / positions + down_bias
    )
    returned = [
        lax.ppermute(
            layer_scale * (block_sums(rows) / positions),
            "rep",
            perm=[(r, (r - k) % n_rep) for r in range(n_rep)],
        )
        for k, rows in enumerate(received, start=1)
    ]
    pooled = own_term
    for term in returned:
        pooled = pooled + term
    embedded = layer_norm(pooled, head_gain, head_bias, 1e-06).astype(jnp.bfloat16)
    embedded_all = lax.all_gather(embedded, "slide", axis=0, tiled=True)

    fresh_normed = project(embedded_all, weight_parts, slide_gain)
    fresh_mixed = normalize_heads(
        jnp.dot(fresh_normed, qkv_weight, preferred_element_type=jnp.float32)
    ).reshape(n_slide, fresh_count, -1)
    local_heads = jnp.concatenate([fresh_mixed, stale_mixed[:, fresh_count:]], axis=1)
    n_slide = local_heads.shape[0]
    seq_len = n_slide * local_heads.shape[1]
    local_heads = local_heads.reshape(seq_len, -1)

    heads_here = local_heads.shape[1] // (3 * HDIM)
    arranged = local_heads.reshape(seq_len, heads_here, 3, HDIM)
    queries = arranged[:, :, 0]
    key_rows = arranged[:, :, 1]
    value_rows = arranged[:, :, 2]
    my_slopes = lax.dynamic_slice_in_dim(
        head_slopes, lax.axis_index("slide") * heads_here, heads_here, 0
    )
    coord_x = tile_coords[0, 0].astype(jnp.float32)
    coord_y = tile_coords[0, 1].astype(jnp.float32)
    valid = valid_counts[0]
    key_ok = jnp.arange(seq_len, dtype=jnp.int32) < valid
    inv_root = 1.0 / math.sqrt(HDIM)

    distance = jnp.abs(coord_x[:, None] - coord_x[None, :]) + jnp.abs(
        coord_y[:, None] - coord_y[None, :]
    )
    scores = (
        jnp.einsum("qhd,khd->hqk", queries, key_rows, preferred_element_type=jnp.float32)
        * inv_root
        - my_slopes[:, None, None] * distance[None]
    )
    weights = jnp.where(key_ok[None, None, :], jnp.exp(scores), 0.0).astype(jnp.bfloat16)
    totals = jnp.sum(weights, axis=-1, dtype=jnp.float32)
    weighted = jnp.einsum("hqk,khd->qhd", weights, value_rows, preferred_element_type=jnp.float32)
    safe = jnp.where(key_ok[None, :], totals, 1.0)
    attended = jnp.where(key_ok[:, None, None], weighted / safe.T[:, :, None], 0.0)
    attended = attended.astype(jnp.bfloat16).reshape(seq_len, heads_here * HDIM)
    context = lax.all_to_all(attended, "slide", split_axis=0, concat_axis=1, tiled=True)
    return (embedded[None], context[None])


def solution(mesh):
    in_specs = (
        P(("groups", "rep", "section"), "slide", None, None),
        P(),
        P(),
        P(),
        P(),
        P(None, "rep"),
        P("rep"),
        P("rep", None),
        P(),
        P(),
        P(),
        P(),
        P(("groups", "rep", "section"), "slide", None),
        P("slide", None),
        P(),
        P(None, "slide"),
        P(),
        P(("groups", "rep", "section"), None, None),
        P(("groups", "rep", "section")),
    )
    out_specs = (
        P(("groups", "rep", "section"), "slide", None),
        P(("groups", "rep", "section"), "slide", None),
    )
    return jax.shard_map(
        on_device, mesh=mesh, in_specs=in_specs, out_specs=out_specs, check_vma=False
    )
```

```python
import math

import jax
import jax.numpy as jnp
from jax import lax
from jax.experimental import pallas as pl
from jax.experimental.pallas import tpu as pltpu
from jax.sharding import PartitionSpec as P

SIDE = 7
KER = 7
HDIM = 64
LANES = 128


def layer_norm(inputs, gain, shift, epsilon):
    center = jnp.mean(inputs, axis=-1, keepdims=True)
    centered = inputs - center
    spread = jnp.mean(centered * centered, axis=-1, keepdims=True)
    return centered * lax.rsqrt(spread + epsilon) * gain + shift


def dw_ln_kernel(x_ref, w_ref, b_ref, g_ref, nb_ref, o_ref, conv_ref):
    C = x_ref.shape[-1]
    jrow = lax.broadcasted_iota(jnp.int32, (8, LANES), 0)
    masks = [((jrow + (bb - 3)) >= 0) & ((jrow + (bb - 3)) < SIDE) for bb in range(KER)]
    def chunk(ci, carry):
        c0 = pl.multiple_of(ci * LANES, LANES)
        rows = [x_ref[0, i, :, pl.ds(c0, LANES)].astype(jnp.float32) for i in range(SIDE)]
        bias = jnp.broadcast_to(b_ref[:, pl.ds(c0, LANES)], (8, LANES))
        acc = [bias for _ in range(SIDE)]
        for ip in range(SIDE):
            for bb in range(KER):
                s = bb - 3
                sh = rows[ip] if s == 0 else pltpu.roll(rows[ip], shift=(-s) % 8, axis=0)
                sh = jnp.where(masks[bb], sh, 0.0)
                for a in range(KER):
                    i = ip - (a - 3)
                    if 0 <= i < SIDE:
                        wv = jnp.broadcast_to(w_ref[pl.ds(a * KER + bb, 1), pl.ds(c0, LANES)], (8, LANES))
                        acc[i] = acc[i] + sh * wv
        for i in range(SIDE):
            conv_ref[i, :, pl.ds(c0, LANES)] = acc[i]
        return carry
    lax.fori_loop(0, C // LANES, chunk, 0)
    g = g_ref[...]
    nb = nb_ref[...]
    for i in range(SIDE):
        v = conv_ref[i]
        mean = jnp.mean(v, axis=-1, keepdims=True)
        cen = v - mean
        var = jnp.mean(cen * cen, axis=-1, keepdims=True)
        o_ref[0, i] = (cen * lax.rsqrt(var + 1e-06) * g + nb).astype(o_ref.dtype)

def dw_ln(tiles, depth_weight, depth_bias, norm_gain, norm_bias):
    T, _, C = tiles.shape
    x = jnp.pad(tiles.reshape(T, SIDE, SIDE, C), ((0, 0), (0, 0), (0, 1), (0, 0)))
    out = pl.pallas_call(
        dw_ln_kernel,
        grid=(T,),
        in_specs=[
            pl.BlockSpec((1, SIDE, 8, C), lambda t: (t, 0, 0, 0)),
            pl.BlockSpec((KER * KER, C), lambda t: (0, 0)),
            pl.BlockSpec((1, C), lambda t: (0, 0)),
            pl.BlockSpec((1, C), lambda t: (0, 0)),
            pl.BlockSpec((1, C), lambda t: (0, 0)),
        ],
        out_specs=pl.BlockSpec((1, SIDE, 8, C), lambda t: (t, 0, 0, 0)),
        out_shape=jax.ShapeDtypeStruct((T, SIDE, 8, C), jnp.bfloat16),
        scratch_shapes=[pltpu.VMEM((SIDE, 8, C), jnp.float32)],
    )(x, depth_weight, depth_bias[None], norm_gain[None], norm_bias[None])
    return out[:, :, :SIDE].reshape(T * SIDE * SIDE, C)


def normalize_heads(values):
    lead = values.shape[:-1]
    grouped = values.reshape(lead + (-1, 3, HDIM))
    paired = grouped[..., :2, :]
    scaled = paired * lax.rsqrt(jnp.mean(paired * paired, axis=-1, keepdims=True) + 1e-06)
    joined = jnp.concatenate([scaled, grouped[..., 2:, :]], axis=-2)
    return joined.astype(jnp.bfloat16).reshape(lead + (-1,))


def project(rows, weight_parts, slide_gain):
    projected = jnp.einsum(
        "nk,skc->nsc", rows, weight_parts, preferred_element_type=jnp.float32
    ).reshape(rows.shape[0], -1)
    return layer_norm(projected, slide_gain, 0.0, 1e-05).astype(jnp.bfloat16)


def on_device(
    tile_features,
    depth_weight,
    depth_bias,
    norm_gain,
    norm_bias,
    up_weight,
    up_bias,
    down_weight,
    down_bias,
    layer_scale,
    head_gain,
    head_bias,
    embed_store,
    in_weight,
    slide_gain,
    qkv_weight,
    head_slopes,
    tile_coords,
    valid_counts,
):
    n_sec = lax.axis_size("section")
    col_part = in_weight.shape[1] // n_sec
    my_cols = lax.dynamic_slice_in_dim(
        in_weight, lax.axis_index("section") * col_part, col_part, 1
    )
    cols_full = lax.all_gather(my_cols, "slide", axis=0, tiled=True)

    tile_data = tile_features[0].astype(jnp.float32)
    fresh_count = tile_data.shape[0]
    n_rep = lax.axis_size("rep")
    my_rep = lax.axis_index("rep")
    n_slide = lax.axis_size("slide")
    my_slide = lax.axis_index("slide")
    normed = dw_ln(tile_features[0], depth_weight, depth_bias, norm_gain, norm_bias)

    def block_sums(rows):
        hidden = jax.nn.gelu(
            jnp.dot(rows, up_weight, preferred_element_type=jnp.float32) + up_bias,
            approximate=False,
        ).astype(jnp.bfloat16)
        part = jnp.dot(hidden, down_weight, preferred_element_type=jnp.float32).astype(
            jnp.bfloat16
        )
        return jnp.sum(part.astype(jnp.float32).reshape(tile_data.shape), axis=1)

    received = [
        lax.ppermute(normed, "rep", perm=[(r, (r + k) % n_rep) for r in range(n_rep)])
        for k in range(1, n_rep)
    ]
    positions = tile_data.shape[1]
    own_term = jnp.mean(tile_data, axis=1) + layer_scale * (
        block_sums(normed) / positions + down_bias
    )
    peer_terms = [layer_scale * (block_sums(rows) / positions) for rows in received]
    cols_full, own_term, peer_terms = lax.optimization_barrier(
        (cols_full, own_term, peer_terms)
    )
    weight_parts = lax.all_gather(cols_full, "section", axis=0, tiled=False)
    returned = [
        lax.ppermute(term, "rep", perm=[(r, (r - k) % n_rep) for r in range(n_rep)])
        for k, term in enumerate(peer_terms, start=1)
    ]
    pooled = own_term
    for term in returned:
        pooled = pooled + term
    embedded = layer_norm(pooled, head_gain, head_bias, 1e-06).astype(jnp.bfloat16)

    seq_rows = jnp.concatenate([embedded, embed_store[0, fresh_count:]], axis=0)
    normed_seq = project(seq_rows, weight_parts, slide_gain)
    normed_all = lax.all_gather(normed_seq, "slide", axis=0, tiled=True)
    local_heads = normalize_heads(
        jnp.dot(normed_all, qkv_weight, preferred_element_type=jnp.float32)
    )
    seq_len = local_heads.shape[0]

    heads_here = local_heads.shape[1] // (3 * HDIM)
    arranged = local_heads.reshape(seq_len, heads_here, 3, HDIM)
    queries = arranged[:, :, 0]
    key_rows = arranged[:, :, 1]
    value_rows = arranged[:, :, 2]
    my_slopes = lax.dynamic_slice_in_dim(
        head_slopes, lax.axis_index("slide") * heads_here, heads_here, 0
    )
    coord_x = tile_coords[0, 0].astype(jnp.float32)
    coord_y = tile_coords[0, 1].astype(jnp.float32)
    valid = valid_counts[0]
    key_ok = jnp.arange(seq_len, dtype=jnp.int32) < valid
    inv_root = 1.0 / math.sqrt(HDIM)

    distance = jnp.abs(coord_x[:, None] - coord_x[None, :]) + jnp.abs(
        coord_y[:, None] - coord_y[None, :]
    )
    scores = (
        jnp.einsum("qhd,khd->hqk", queries, key_rows, preferred_element_type=jnp.float32)
        * inv_root
        - my_slopes[:, None, None] * distance[None]
    )
    weights = jnp.where(key_ok[None, None, :], jnp.exp(scores), 0.0).astype(jnp.bfloat16)
    totals = jnp.sum(weights, axis=-1, dtype=jnp.float32)
    weighted = jnp.einsum("hqk,khd->qhd", weights, value_rows, preferred_element_type=jnp.float32)
    safe = jnp.where(key_ok[None, :], totals, 1.0)
    attended = jnp.where(key_ok[:, None, None], weighted / safe.T[:, :, None], 0.0)
    attended = attended.astype(jnp.bfloat16).reshape(seq_len, heads_here * HDIM)
    context = lax.all_to_all(attended, "slide", split_axis=0, concat_axis=1, tiled=True)
    return (embedded[None], context[None])


def solution(mesh):
    in_specs = (
        P(("groups", "rep", "section"), "slide", None, None),
        P(),
        P(),
        P(),
        P(),
        P(None, "rep"),
        P("rep"),
        P("rep", None),
        P(),
        P(),
        P(),
        P(),
        P(("groups", "rep", "section"), "slide", None),
        P("slide", None),
        P(),
        P(None, "slide"),
        P(),
        P(("groups", "rep", "section"), None, None),
        P(("groups", "rep", "section")),
    )
    out_specs = (
        P(("groups", "rep", "section"), "slide", None),
        P(("groups", "rep", "section"), "slide", None),
    )
    return jax.shard_map(
        on_device, mesh=mesh, in_specs=in_specs, out_specs=out_specs, check_vma=False
    )
```

```python
import math

import jax
import jax.numpy as jnp
from jax import lax
from jax.experimental import pallas as pl
from jax.experimental.pallas import tpu as pltpu
from jax.sharding import PartitionSpec as P

SIDE = 7
KER = 7
HDIM = 64
LANES = 128


def layer_norm(inputs, gain, shift, epsilon):
    center = jnp.mean(inputs, axis=-1, keepdims=True)
    centered = inputs - center
    spread = jnp.mean(centered * centered, axis=-1, keepdims=True)
    return centered * lax.rsqrt(spread + epsilon) * gain + shift


def dw_ln_kernel(x_ref, w_ref, b_ref, g_ref, nb_ref, o_ref, conv_ref):
    C = x_ref.shape[-1]
    jrow = lax.broadcasted_iota(jnp.int32, (8, LANES), 0)
    masks = [((jrow + (bb - 3)) >= 0) & ((jrow + (bb - 3)) < SIDE) for bb in range(KER)]
    def chunk(ci, carry):
        c0 = pl.multiple_of(ci * LANES, LANES)
        rows = [x_ref[0, i, :, pl.ds(c0, LANES)].astype(jnp.float32) for i in range(SIDE)]
        bias = jnp.broadcast_to(b_ref[:, pl.ds(c0, LANES)], (8, LANES))
        acc = [bias for _ in range(SIDE)]
        for ip in range(SIDE):
            for bb in range(KER):
                s = bb - 3
                sh = rows[ip] if s == 0 else pltpu.roll(rows[ip], shift=(-s) % 8, axis=0)
                sh = jnp.where(masks[bb], sh, 0.0)
                for a in range(KER):
                    i = ip - (a - 3)
                    if 0 <= i < SIDE:
                        wv = jnp.broadcast_to(w_ref[pl.ds(a * KER + bb, 1), pl.ds(c0, LANES)], (8, LANES))
                        acc[i] = acc[i] + sh * wv
        for i in range(SIDE):
            conv_ref[i, :, pl.ds(c0, LANES)] = acc[i]
        return carry
    lax.fori_loop(0, C // LANES, chunk, 0)
    g = g_ref[...]
    nb = nb_ref[...]
    for i in range(SIDE):
        v = conv_ref[i]
        mean = jnp.mean(v, axis=-1, keepdims=True)
        cen = v - mean
        var = jnp.mean(cen * cen, axis=-1, keepdims=True)
        o_ref[0, i] = (cen * lax.rsqrt(var + 1e-06) * g + nb).astype(o_ref.dtype)

def dw_ln(tiles, depth_weight, depth_bias, norm_gain, norm_bias):
    T, _, C = tiles.shape
    x = jnp.pad(tiles.reshape(T, SIDE, SIDE, C), ((0, 0), (0, 0), (0, 1), (0, 0)))
    out = pl.pallas_call(
        dw_ln_kernel,
        grid=(T,),
        in_specs=[
            pl.BlockSpec((1, SIDE, 8, C), lambda t: (t, 0, 0, 0)),
            pl.BlockSpec((KER * KER, C), lambda t: (0, 0)),
            pl.BlockSpec((1, C), lambda t: (0, 0)),
            pl.BlockSpec((1, C), lambda t: (0, 0)),
            pl.BlockSpec((1, C), lambda t: (0, 0)),
        ],
        out_specs=pl.BlockSpec((1, SIDE, 8, C), lambda t: (t, 0, 0, 0)),
        out_shape=jax.ShapeDtypeStruct((T, SIDE, 8, C), jnp.bfloat16),
        scratch_shapes=[pltpu.VMEM((SIDE, 8, C), jnp.float32)],
    )(x, depth_weight, depth_bias[None], norm_gain[None], norm_bias[None])
    return out[:, :, :SIDE].reshape(T * SIDE * SIDE, C)


def normalize_heads(values):
    lead = values.shape[:-1]
    grouped = values.reshape(lead + (-1, 3, HDIM))
    paired = grouped[..., :2, :]
    scaled = paired * lax.rsqrt(jnp.mean(paired * paired, axis=-1, keepdims=True) + 1e-06)
    joined = jnp.concatenate([scaled, grouped[..., 2:, :]], axis=-2)
    return joined.astype(jnp.bfloat16).reshape(lead + (-1,))


def line_gather(block, axis_name):
    n = lax.axis_size(axis_name)
    me = lax.axis_index(axis_name)
    right = block
    left = block
    entries = [block]
    for _ in range(1, n):
        right = lax.ppermute(right, axis_name, [(j, j + 1) for j in range(n - 1)])
        left = lax.ppermute(left, axis_name, [(j, j - 1) for j in range(1, n)])
        entries += [right, left]
    source = jnp.arange(n, dtype=jnp.int32)
    pick = jnp.where(
        source == me, 0, jnp.where(source < me, 2 * (me - source) - 1, 2 * (source - me))
    )
    return jnp.take(jnp.stack(entries), pick, axis=0)


def project(rows, weight_parts, slide_gain):
    mine, other, first = weight_parts
    mine_part = jnp.dot(rows, mine, preferred_element_type=jnp.float32)
    other_part = jnp.dot(rows, other, preferred_element_type=jnp.float32)
    projected = jnp.where(
        first,
        jnp.concatenate([mine_part, other_part], axis=-1),
        jnp.concatenate([other_part, mine_part], axis=-1),
    )
    return layer_norm(projected, slide_gain, 0.0, 1e-05).astype(jnp.bfloat16)


def on_device(
    tile_features,
    depth_weight,
    depth_bias,
    norm_gain,
    norm_bias,
    up_weight,
    up_bias,
    down_weight,
    down_bias,
    layer_scale,
    head_gain,
    head_bias,
    embed_store,
    in_weight,
    slide_gain,
    qkv_weight,
    head_slopes,
    tile_coords,
    valid_counts,
):
    n_sec = lax.axis_size("section")
    col_part = in_weight.shape[1] // n_sec
    my_cols = lax.dynamic_slice_in_dim(
        in_weight, lax.axis_index("section") * col_part, col_part, 1
    )
    cols_full = lax.all_gather(my_cols, "slide", axis=0, tiled=True)

    stored_all = line_gather(embed_store[0], "slide")

    tile_data = tile_features[0].astype(jnp.float32)
    fresh_count = tile_data.shape[0]
    n_rep = lax.axis_size("rep")
    my_rep = lax.axis_index("rep")
    n_slide = lax.axis_size("slide")
    my_slide = lax.axis_index("slide")
    normed = dw_ln(tile_features[0], depth_weight, depth_bias, norm_gain, norm_bias)

    def block_sums(rows):
        hidden = jax.nn.gelu(
            jnp.dot(rows, up_weight, preferred_element_type=jnp.float32) + up_bias,
            approximate=False,
        ).astype(jnp.bfloat16)
        part = jnp.dot(hidden, down_weight, preferred_element_type=jnp.float32).astype(
            jnp.bfloat16
        )
        return jnp.sum(part.astype(jnp.float32).reshape(tile_data.shape), axis=1)

    received = [
        lax.ppermute(normed, "rep", perm=[(r, (r + k) % n_rep) for r in range(n_rep)])
        for k in range(1, n_rep)
    ]
    positions = tile_data.shape[1]
    own_term = jnp.mean(tile_data, axis=1) + layer_scale * (
        block_sums(normed) / positions + down_bias
    )
    peer_terms = [layer_scale * (block_sums(rows) / positions) for rows in received]
    cols_full, own_term, peer_terms = lax.optimization_barrier(
        (cols_full, own_term, peer_terms)
    )
    other_cols = lax.ppermute(
        cols_full, "section", perm=[(c, (c + 1) % n_sec) for c in range(n_sec)]
    )
    first = lax.axis_index("section") == 0
    weight_parts = (cols_full, other_cols, first)
    returned = [
        lax.ppermute(term, "rep", perm=[(r, (r - k) % n_rep) for r in range(n_rep)])
        for k, term in enumerate(peer_terms, start=1)
    ]
    pooled = own_term
    for term in returned:
        pooled = pooled + term
    embedded = layer_norm(pooled, head_gain, head_bias, 1e-06).astype(jnp.bfloat16)

    embedded_all = lax.all_gather(embedded, "slide", axis=0, tiled=False)
    seq_rows = jnp.concatenate([embedded_all, stored_all[:, fresh_count:]], axis=1)
    normed_all = project(seq_rows.reshape(-1, seq_rows.shape[-1]), weight_parts, slide_gain)
    local_heads = normalize_heads(
        jnp.dot(normed_all, qkv_weight, preferred_element_type=jnp.float32)
    )
    seq_len = local_heads.shape[0]

    heads_here = local_heads.shape[1] // (3 * HDIM)
    arranged = local_heads.reshape(seq_len, heads_here, 3, HDIM)
    queries = arranged[:, :, 0]
    key_rows = arranged[:, :, 1]
    value_rows = arranged[:, :, 2]
    my_slopes = lax.dynamic_slice_in_dim(
        head_slopes, lax.axis_index("slide") * heads_here, heads_here, 0
    )
    coord_x = tile_coords[0, 0].astype(jnp.float32)
    coord_y = tile_coords[0, 1].astype(jnp.float32)
    valid = valid_counts[0]
    key_ok = jnp.arange(seq_len, dtype=jnp.int32) < valid
    inv_root = 1.0 / math.sqrt(HDIM)

    distance = jnp.abs(coord_x[:, None] - coord_x[None, :]) + jnp.abs(
        coord_y[:, None] - coord_y[None, :]
    )
    scores = (
        jnp.einsum("qhd,khd->hqk", queries, key_rows, preferred_element_type=jnp.float32)
        * inv_root
        - my_slopes[:, None, None] * distance[None]
    )
    weights = jnp.where(key_ok[None, None, :], jnp.exp(scores), 0.0).astype(jnp.bfloat16)
    totals = jnp.sum(weights, axis=-1, dtype=jnp.float32)
    weighted = jnp.einsum("hqk,khd->qhd", weights, value_rows, preferred_element_type=jnp.float32)
    safe = jnp.where(key_ok[None, :], totals, 1.0)
    attended = jnp.where(key_ok[:, None, None], weighted / safe.T[:, :, None], 0.0)
    attended = attended.astype(jnp.bfloat16).reshape(seq_len, heads_here * HDIM)
    context = lax.all_to_all(attended, "slide", split_axis=0, concat_axis=1, tiled=True)
    return (embedded[None], context[None])


def solution(mesh):
    in_specs = (
        P(("groups", "rep", "section"), "slide", None, None),
        P(),
        P(),
        P(),
        P(),
        P(None, "rep"),
        P("rep"),
        P("rep", None),
        P(),
        P(),
        P(),
        P(),
        P(("groups", "rep", "section"), "slide", None),
        P("slide", None),
        P(),
        P(None, "slide"),
        P(),
        P(("groups", "rep", "section"), None, None),
        P(("groups", "rep", "section")),
    )
    out_specs = (
        P(("groups", "rep", "section"), "slide", None),
        P(("groups", "rep", "section"), "slide", None),
    )
    return jax.shard_map(
        on_device, mesh=mesh, in_specs=in_specs, out_specs=out_specs, check_vma=False
    )
```

```python
import math

import jax
import jax.numpy as jnp
from jax import lax
from jax.experimental import pallas as pl
from jax.experimental.pallas import tpu as pltpu
from jax.sharding import PartitionSpec as P

SIDE = 7
KER = 7
HDIM = 64
LANES = 128


def layer_norm(inputs, gain, shift, epsilon):
    center = jnp.mean(inputs, axis=-1, keepdims=True)
    centered = inputs - center
    spread = jnp.mean(centered * centered, axis=-1, keepdims=True)
    return centered * lax.rsqrt(spread + epsilon) * gain + shift


def dw_ln_kernel(x_ref, w_ref, b_ref, g_ref, nb_ref, o_ref, conv_ref):
    C = x_ref.shape[-1]
    jrow = lax.broadcasted_iota(jnp.int32, (8, LANES), 0)
    masks = [((jrow + (bb - 3)) >= 0) & ((jrow + (bb - 3)) < SIDE) for bb in range(KER)]
    def chunk(ci, carry):
        c0 = pl.multiple_of(ci * LANES, LANES)
        rows = [x_ref[0, i, :, pl.ds(c0, LANES)].astype(jnp.float32) for i in range(SIDE)]
        bias = jnp.broadcast_to(b_ref[:, pl.ds(c0, LANES)], (8, LANES))
        acc = [bias for _ in range(SIDE)]
        for ip in range(SIDE):
            for bb in range(KER):
                s = bb - 3
                sh = rows[ip] if s == 0 else pltpu.roll(rows[ip], shift=(-s) % 8, axis=0)
                sh = jnp.where(masks[bb], sh, 0.0)
                for a in range(KER):
                    i = ip - (a - 3)
                    if 0 <= i < SIDE:
                        wv = jnp.broadcast_to(w_ref[pl.ds(a * KER + bb, 1), pl.ds(c0, LANES)], (8, LANES))
                        acc[i] = acc[i] + sh * wv
        for i in range(SIDE):
            conv_ref[i, :, pl.ds(c0, LANES)] = acc[i]
        return carry
    lax.fori_loop(0, C // LANES, chunk, 0)
    g = g_ref[...]
    nb = nb_ref[...]
    for i in range(SIDE):
        v = conv_ref[i]
        mean = jnp.mean(v, axis=-1, keepdims=True)
        cen = v - mean
        var = jnp.mean(cen * cen, axis=-1, keepdims=True)
        o_ref[0, i] = (cen * lax.rsqrt(var + 1e-06) * g + nb).astype(o_ref.dtype)

def dw_ln(tiles, depth_weight, depth_bias, norm_gain, norm_bias):
    T, _, C = tiles.shape
    x = jnp.pad(tiles.reshape(T, SIDE, SIDE, C), ((0, 0), (0, 0), (0, 1), (0, 0)))
    out = pl.pallas_call(
        dw_ln_kernel,
        grid=(T,),
        in_specs=[
            pl.BlockSpec((1, SIDE, 8, C), lambda t: (t, 0, 0, 0)),
            pl.BlockSpec((KER * KER, C), lambda t: (0, 0)),
            pl.BlockSpec((1, C), lambda t: (0, 0)),
            pl.BlockSpec((1, C), lambda t: (0, 0)),
            pl.BlockSpec((1, C), lambda t: (0, 0)),
        ],
        out_specs=pl.BlockSpec((1, SIDE, 8, C), lambda t: (t, 0, 0, 0)),
        out_shape=jax.ShapeDtypeStruct((T, SIDE, 8, C), jnp.bfloat16),
        scratch_shapes=[pltpu.VMEM((SIDE, 8, C), jnp.float32)],
    )(x, depth_weight, depth_bias[None], norm_gain[None], norm_bias[None])
    return out[:, :, :SIDE].reshape(T * SIDE * SIDE, C)


def normalize_heads(values):
    lead = values.shape[:-1]
    grouped = values.reshape(lead + (-1, 3, HDIM))
    paired = grouped[..., :2, :]
    scaled = paired * lax.rsqrt(jnp.mean(paired * paired, axis=-1, keepdims=True) + 1e-06)
    joined = jnp.concatenate([scaled, grouped[..., 2:, :]], axis=-2)
    return joined.astype(jnp.bfloat16).reshape(lead + (-1,))


def project(rows, weight_parts, slide_gain):
    mine, other, first = weight_parts
    mine_part = jnp.dot(rows, mine, preferred_element_type=jnp.float32)
    other_part = jnp.dot(rows, other, preferred_element_type=jnp.float32)
    projected = jnp.where(
        first,
        jnp.concatenate([mine_part, other_part], axis=-1),
        jnp.concatenate([other_part, mine_part], axis=-1),
    )
    return layer_norm(projected, slide_gain, 0.0, 1e-05).astype(jnp.bfloat16)


def on_device(
    tile_features,
    depth_weight,
    depth_bias,
    norm_gain,
    norm_bias,
    up_weight,
    up_bias,
    down_weight,
    down_bias,
    layer_scale,
    head_gain,
    head_bias,
    embed_store,
    in_weight,
    slide_gain,
    qkv_weight,
    head_slopes,
    tile_coords,
    valid_counts,
):
    n_sec = lax.axis_size("section")
    col_part = in_weight.shape[1] // n_sec
    my_cols = lax.dynamic_slice_in_dim(
        in_weight, lax.axis_index("section") * col_part, col_part, 1
    )
    cols_full = lax.all_gather(my_cols, "slide", axis=0, tiled=True)

    tile_data = tile_features[0].astype(jnp.float32)
    fresh_count = tile_data.shape[0]
    n_rep = lax.axis_size("rep")
    my_rep = lax.axis_index("rep")
    n_slide = lax.axis_size("slide")
    my_slide = lax.axis_index("slide")
    normed = dw_ln(tile_features[0], depth_weight, depth_bias, norm_gain, norm_bias)

    def block_sums(rows):
        hidden = jax.nn.gelu(
            jnp.dot(rows, up_weight, preferred_element_type=jnp.float32) + up_bias,
            approximate=False,
        ).astype(jnp.bfloat16)
        part = jnp.dot(hidden, down_weight, preferred_element_type=jnp.float32).astype(
            jnp.bfloat16
        )
        return jnp.sum(part.astype(jnp.float32).reshape(tile_data.shape), axis=1)

    received = [
        lax.ppermute(normed, "rep", perm=[(r, (r + k) % n_rep) for r in range(n_rep)])
        for k in range(1, n_rep)
    ]
    positions = tile_data.shape[1]
    own_term = jnp.mean(tile_data, axis=1) + layer_scale * (
        block_sums(normed) / positions + down_bias
    )
    peer_terms = [layer_scale * (block_sums(rows) / positions) for rows in received]
    cols_full, own_term, peer_terms = lax.optimization_barrier(
        (cols_full, own_term, peer_terms)
    )
    other_cols = lax.ppermute(
        cols_full, "section", perm=[(c, (c + 1) % n_sec) for c in range(n_sec)]
    )
    first = lax.axis_index("section") == 0
    weight_parts = (cols_full, other_cols, first)
    returned = [
        lax.ppermute(term, "rep", perm=[(r, (r - k) % n_rep) for r in range(n_rep)])
        for k, term in enumerate(peer_terms, start=1)
    ]
    pooled = own_term
    for term in returned:
        pooled = pooled + term
    embedded = layer_norm(pooled, head_gain, head_bias, 1e-06).astype(jnp.bfloat16)

    seq_rows = jnp.concatenate([embedded, embed_store[0, fresh_count:]], axis=0)
    normed_seq = project(seq_rows, weight_parts, slide_gain)
    normed_all = lax.all_gather(normed_seq, "slide", axis=0, tiled=True)
    local_heads = normalize_heads(
        jnp.dot(normed_all, qkv_weight, preferred_element_type=jnp.float32)
    )
    seq_len = local_heads.shape[0]

    heads_here = local_heads.shape[1] // (3 * HDIM)
    arranged = local_heads.reshape(seq_len, heads_here, 3, HDIM)
    queries = arranged[:, :, 0]
    key_rows = arranged[:, :, 1]
    value_rows = arranged[:, :, 2]
    my_slopes = lax.dynamic_slice_in_dim(
        head_slopes, lax.axis_index("slide") * heads_here, heads_here, 0
    )
    coord_x = tile_coords[0, 0].astype(jnp.float32)
    coord_y = tile_coords[0, 1].astype(jnp.float32)
    valid = valid_counts[0]
    key_ok = jnp.arange(seq_len, dtype=jnp.int32) < valid
    inv_root = 1.0 / math.sqrt(HDIM)

    distance = jnp.abs(coord_x[:, None] - coord_x[None, :]) + jnp.abs(
        coord_y[:, None] - coord_y[None, :]
    )
    scores = (
        jnp.einsum("qhd,khd->hqk", queries, key_rows, preferred_element_type=jnp.float32)
        * inv_root
        - my_slopes[:, None, None] * distance[None]
    )
    weights = jnp.where(key_ok[None, None, :], jnp.exp(scores), 0.0).astype(jnp.bfloat16)
    totals = jnp.sum(weights, axis=-1, dtype=jnp.float32)
    weighted = jnp.einsum("hqk,khd->qhd", weights, value_rows, preferred_element_type=jnp.float32)
    safe = jnp.where(key_ok[None, :], totals, 1.0)
    attended = jnp.where(key_ok[:, None, None], weighted / safe.T[:, :, None], 0.0)
    attended = attended.astype(jnp.bfloat16).reshape(seq_len, heads_here * HDIM)
    context = lax.all_to_all(attended, "slide", split_axis=0, concat_axis=1, tiled=True)
    return (embedded[None], context[None])


def solution(mesh):
    in_specs = (
        P(("groups", "rep", "section"), "slide", None, None),
        P(),
        P(),
        P(),
        P(),
        P(None, "rep"),
        P("rep"),
        P("rep", None),
        P(),
        P(),
        P(),
        P(),
        P(("groups", "rep", "section"), "slide", None),
        P("slide", None),
        P(),
        P(None, "slide"),
        P(),
        P(("groups", "rep", "section"), None, None),
        P(("groups", "rep", "section")),
    )
    out_specs = (
        P(("groups", "rep", "section"), "slide", None),
        P(("groups", "rep", "section"), "slide", None),
    )
    return jax.shard_map(
        on_device, mesh=mesh, in_specs=in_specs, out_specs=out_specs, check_vma=False
    )
```

```python
import math

import jax
import jax.numpy as jnp
from jax import lax
from jax.experimental import pallas as pl
from jax.experimental.pallas import tpu as pltpu
from jax.sharding import PartitionSpec as P

SIDE = 7
KER = 7
HDIM = 64
LANES = 128


def layer_norm(inputs, gain, shift, epsilon):
    center = jnp.mean(inputs, axis=-1, keepdims=True)
    centered = inputs - center
    spread = jnp.mean(centered * centered, axis=-1, keepdims=True)
    return centered * lax.rsqrt(spread + epsilon) * gain + shift


def dw_ln_kernel(x_ref, w_ref, b_ref, g_ref, nb_ref, o_ref, conv_ref):
    C = x_ref.shape[-1]
    jrow = lax.broadcasted_iota(jnp.int32, (8, LANES), 0)
    masks = [((jrow + (bb - 3)) >= 0) & ((jrow + (bb - 3)) < SIDE) for bb in range(KER)]
    def chunk(ci, carry):
        c0 = pl.multiple_of(ci * LANES, LANES)
        rows = [x_ref[0, i, :, pl.ds(c0, LANES)].astype(jnp.float32) for i in range(SIDE)]
        bias = jnp.broadcast_to(b_ref[:, pl.ds(c0, LANES)], (8, LANES))
        acc = [bias for _ in range(SIDE)]
        for ip in range(SIDE):
            for bb in range(KER):
                s = bb - 3
                sh = rows[ip] if s == 0 else pltpu.roll(rows[ip], shift=(-s) % 8, axis=0)
                sh = jnp.where(masks[bb], sh, 0.0)
                for a in range(KER):
                    i = ip - (a - 3)
                    if 0 <= i < SIDE:
                        wv = jnp.broadcast_to(w_ref[pl.ds(a * KER + bb, 1), pl.ds(c0, LANES)], (8, LANES))
                        acc[i] = acc[i] + sh * wv
        for i in range(SIDE):
            conv_ref[i, :, pl.ds(c0, LANES)] = acc[i]
        return carry
    lax.fori_loop(0, C // LANES, chunk, 0)
    g = g_ref[...]
    nb = nb_ref[...]
    for i in range(SIDE):
        v = conv_ref[i]
        mean = jnp.mean(v, axis=-1, keepdims=True)
        cen = v - mean
        var = jnp.mean(cen * cen, axis=-1, keepdims=True)
        o_ref[0, i] = (cen * lax.rsqrt(var + 1e-06) * g + nb).astype(o_ref.dtype)

def dw_ln(tiles, depth_weight, depth_bias, norm_gain, norm_bias):
    T, _, C = tiles.shape
    x = jnp.pad(tiles.reshape(T, SIDE, SIDE, C), ((0, 0), (0, 0), (0, 1), (0, 0)))
    out = pl.pallas_call(
        dw_ln_kernel,
        grid=(T,),
        in_specs=[
            pl.BlockSpec((1, SIDE, 8, C), lambda t: (t, 0, 0, 0)),
            pl.BlockSpec((KER * KER, C), lambda t: (0, 0)),
            pl.BlockSpec((1, C), lambda t: (0, 0)),
            pl.BlockSpec((1, C), lambda t: (0, 0)),
            pl.BlockSpec((1, C), lambda t: (0, 0)),
        ],
        out_specs=pl.BlockSpec((1, SIDE, 8, C), lambda t: (t, 0, 0, 0)),
        out_shape=jax.ShapeDtypeStruct((T, SIDE, 8, C), jnp.bfloat16),
        scratch_shapes=[pltpu.VMEM((SIDE, 8, C), jnp.float32)],
    )(x, depth_weight, depth_bias[None], norm_gain[None], norm_bias[None])
    return out[:, :, :SIDE].reshape(T * SIDE * SIDE, C)


def normalize_heads(values):
    lead = values.shape[:-1]
    grouped = values.reshape(lead + (-1, 3, HDIM))
    paired = grouped[..., :2, :]
    scaled = paired * lax.rsqrt(jnp.mean(paired * paired, axis=-1, keepdims=True) + 1e-06)
    joined = jnp.concatenate([scaled, grouped[..., 2:, :]], axis=-2)
    return joined.astype(jnp.bfloat16).reshape(lead + (-1,))


def project(rows, weight_parts, slide_gain):
    mine, other, first = weight_parts
    mine_part = jnp.dot(rows, mine, preferred_element_type=jnp.float32)
    other_part = jnp.dot(rows, other, preferred_element_type=jnp.float32)
    projected = jnp.where(
        first,
        jnp.concatenate([mine_part, other_part], axis=-1),
        jnp.concatenate([other_part, mine_part], axis=-1),
    )
    return layer_norm(projected, slide_gain, 0.0, 1e-05).astype(jnp.bfloat16)


def on_device(
    tile_features,
    depth_weight,
    depth_bias,
    norm_gain,
    norm_bias,
    up_weight,
    up_bias,
    down_weight,
    down_bias,
    layer_scale,
    head_gain,
    head_bias,
    embed_store,
    in_weight,
    slide_gain,
    qkv_weight,
    head_slopes,
    tile_coords,
    valid_counts,
):
    n_sec = lax.axis_size("section")
    col_part = in_weight.shape[1] // n_sec
    my_cols = lax.dynamic_slice_in_dim(
        in_weight, lax.axis_index("section") * col_part, col_part, 1
    )
    cols_full = lax.all_gather(my_cols, "slide", axis=0, tiled=True)

    tile_data = tile_features[0].astype(jnp.float32)
    fresh_count = tile_data.shape[0]
    n_rep = lax.axis_size("rep")
    my_rep = lax.axis_index("rep")
    n_slide = lax.axis_size("slide")
    my_slide = lax.axis_index("slide")
    normed = dw_ln(tile_features[0], depth_weight, depth_bias, norm_gain, norm_bias)

    def block_sums(rows):
        hidden = jax.nn.gelu(
            jnp.dot(rows, up_weight, preferred_element_type=jnp.float32) + up_bias,
            approximate=False,
        ).astype(jnp.bfloat16)
        part = jnp.dot(hidden, down_weight, preferred_element_type=jnp.float32).astype(
            jnp.bfloat16
        )
        return jnp.sum(part.astype(jnp.float32).reshape(tile_data.shape), axis=1)

    received = [
        lax.ppermute(normed, "rep", perm=[(r, (r + k) % n_rep) for r in range(n_rep)])
        for k in range(1, n_rep)
    ]
    positions = tile_data.shape[1]
    own_term = jnp.mean(tile_data, axis=1) + layer_scale * (
        block_sums(normed) / positions + down_bias
    )
    peer_terms = [layer_scale * (block_sums(rows) / positions) for rows in received]
    returned = [
        lax.ppermute(term, "rep", perm=[(r, (r - k) % n_rep) for r in range(n_rep)])
        for k, term in enumerate(peer_terms, start=1)
    ]
    pooled = own_term
    for term in returned:
        pooled = pooled + term
    embedded = layer_norm(pooled, head_gain, head_bias, 1e-06).astype(jnp.bfloat16)
    cols_full, embedded = lax.optimization_barrier((cols_full, embedded))
    other_cols = lax.ppermute(
        cols_full, "section", perm=[(c, (c + 1) % n_sec) for c in range(n_sec)]
    )
    first = lax.axis_index("section") == 0
    weight_parts = (cols_full, other_cols, first)

    seq_rows = jnp.concatenate([embedded, embed_store[0, fresh_count:]], axis=0)
    normed_seq = project(seq_rows, weight_parts, slide_gain)
    normed_all = lax.all_gather(normed_seq, "slide", axis=0, tiled=True)
    local_heads = normalize_heads(
        jnp.dot(normed_all, qkv_weight, preferred_element_type=jnp.float32)
    )
    seq_len = local_heads.shape[0]

    heads_here = local_heads.shape[1] // (3 * HDIM)
    arranged = local_heads.reshape(seq_len, heads_here, 3, HDIM)
    queries = arranged[:, :, 0]
    key_rows = arranged[:, :, 1]
    value_rows = arranged[:, :, 2]
    my_slopes = lax.dynamic_slice_in_dim(
        head_slopes, lax.axis_index("slide") * heads_here, heads_here, 0
    )
    coord_x = tile_coords[0, 0].astype(jnp.float32)
    coord_y = tile_coords[0, 1].astype(jnp.float32)
    valid = valid_counts[0]
    key_ok = jnp.arange(seq_len, dtype=jnp.int32) < valid
    inv_root = 1.0 / math.sqrt(HDIM)

    distance = jnp.abs(coord_x[:, None] - coord_x[None, :]) + jnp.abs(
        coord_y[:, None] - coord_y[None, :]
    )
    scores = (
        jnp.einsum("qhd,khd->hqk", queries, key_rows, preferred_element_type=jnp.float32)
        * inv_root
        - my_slopes[:, None, None] * distance[None]
    )
    weights = jnp.where(key_ok[None, None, :], jnp.exp(scores), 0.0).astype(jnp.bfloat16)
    totals = jnp.sum(weights, axis=-1, dtype=jnp.float32)
    weighted = jnp.einsum("hqk,khd->qhd", weights, value_rows, preferred_element_type=jnp.float32)
    safe = jnp.where(key_ok[None, :], totals, 1.0)
    attended = jnp.where(key_ok[:, None, None], weighted / safe.T[:, :, None], 0.0)
    attended = attended.astype(jnp.bfloat16).reshape(seq_len, heads_here * HDIM)
    context = lax.all_to_all(attended, "slide", split_axis=0, concat_axis=1, tiled=True)
    return (embedded[None], context[None])


def solution(mesh):
    in_specs = (
        P(("groups", "rep", "section"), "slide", None, None),
        P(),
        P(),
        P(),
        P(),
        P(None, "rep"),
        P("rep"),
        P("rep", None),
        P(),
        P(),
        P(),
        P(),
        P(("groups", "rep", "section"), "slide", None),
        P("slide", None),
        P(),
        P(None, "slide"),
        P(),
        P(("groups", "rep", "section"), None, None),
        P(("groups", "rep", "section")),
    )
    out_specs = (
        P(("groups", "rep", "section"), "slide", None),
        P(("groups", "rep", "section"), "slide", None),
    )
    return jax.shard_map(
        on_device, mesh=mesh, in_specs=in_specs, out_specs=out_specs, check_vma=False
    )
```

```python
import math

import jax
import jax.numpy as jnp
from jax import lax
from jax.experimental import pallas as pl
from jax.experimental.pallas import tpu as pltpu
from jax.sharding import PartitionSpec as P

SIDE = 7
KER = 7
HDIM = 64
LANES = 128


def layer_norm(inputs, gain, shift, epsilon):
    center = jnp.mean(inputs, axis=-1, keepdims=True)
    centered = inputs - center
    spread = jnp.mean(centered * centered, axis=-1, keepdims=True)
    return centered * lax.rsqrt(spread + epsilon) * gain + shift


def dw_ln_kernel(x_ref, w_ref, b_ref, g_ref, nb_ref, o_ref, conv_ref):
    C = x_ref.shape[-1]
    jrow = lax.broadcasted_iota(jnp.int32, (8, LANES), 0)
    masks = [((jrow + (bb - 3)) >= 0) & ((jrow + (bb - 3)) < SIDE) for bb in range(KER)]
    def chunk(ci, carry):
        c0 = pl.multiple_of(ci * LANES, LANES)
        rows = [x_ref[0, i, :, pl.ds(c0, LANES)].astype(jnp.float32) for i in range(SIDE)]
        bias = jnp.broadcast_to(b_ref[:, pl.ds(c0, LANES)], (8, LANES))
        acc = [bias for _ in range(SIDE)]
        for ip in range(SIDE):
            for bb in range(KER):
                s = bb - 3
                sh = rows[ip] if s == 0 else pltpu.roll(rows[ip], shift=(-s) % 8, axis=0)
                sh = jnp.where(masks[bb], sh, 0.0)
                for a in range(KER):
                    i = ip - (a - 3)
                    if 0 <= i < SIDE:
                        wv = jnp.broadcast_to(w_ref[pl.ds(a * KER + bb, 1), pl.ds(c0, LANES)], (8, LANES))
                        acc[i] = acc[i] + sh * wv
        for i in range(SIDE):
            conv_ref[i, :, pl.ds(c0, LANES)] = acc[i]
        return carry
    lax.fori_loop(0, C // LANES, chunk, 0)
    g = g_ref[...]
    nb = nb_ref[...]
    for i in range(SIDE):
        v = conv_ref[i]
        mean = jnp.mean(v, axis=-1, keepdims=True)
        cen = v - mean
        var = jnp.mean(cen * cen, axis=-1, keepdims=True)
        o_ref[0, i] = (cen * lax.rsqrt(var + 1e-06) * g + nb).astype(o_ref.dtype)

def dw_ln(tiles, depth_weight, depth_bias, norm_gain, norm_bias):
    T, _, C = tiles.shape
    x = jnp.pad(tiles.reshape(T, SIDE, SIDE, C), ((0, 0), (0, 0), (0, 1), (0, 0)))
    out = pl.pallas_call(
        dw_ln_kernel,
        grid=(T,),
        in_specs=[
            pl.BlockSpec((1, SIDE, 8, C), lambda t: (t, 0, 0, 0)),
            pl.BlockSpec((KER * KER, C), lambda t: (0, 0)),
            pl.BlockSpec((1, C), lambda t: (0, 0)),
            pl.BlockSpec((1, C), lambda t: (0, 0)),
            pl.BlockSpec((1, C), lambda t: (0, 0)),
        ],
        out_specs=pl.BlockSpec((1, SIDE, 8, C), lambda t: (t, 0, 0, 0)),
        out_shape=jax.ShapeDtypeStruct((T, SIDE, 8, C), jnp.bfloat16),
        scratch_shapes=[pltpu.VMEM((SIDE, 8, C), jnp.float32)],
    )(x, depth_weight, depth_bias[None], norm_gain[None], norm_bias[None])
    return out[:, :, :SIDE].reshape(T * SIDE * SIDE, C)


def normalize_heads(values):
    lead = values.shape[:-1]
    grouped = values.reshape(lead + (-1, 3, HDIM))
    paired = grouped[..., :2, :]
    scaled = paired * lax.rsqrt(jnp.mean(paired * paired, axis=-1, keepdims=True) + 1e-06)
    joined = jnp.concatenate([scaled, grouped[..., 2:, :]], axis=-2)
    return joined.astype(jnp.bfloat16).reshape(lead + (-1,))


def project(rows, weight_parts, slide_gain):
    mine, other, first = weight_parts
    mine_part = jnp.dot(rows, mine, preferred_element_type=jnp.float32)
    other_part = jnp.dot(rows, other, preferred_element_type=jnp.float32)
    projected = jnp.where(
        first,
        jnp.concatenate([mine_part, other_part], axis=-1),
        jnp.concatenate([other_part, mine_part], axis=-1),
    )
    return layer_norm(projected, slide_gain, 0.0, 1e-05).astype(jnp.bfloat16)


def on_device(
    tile_features,
    depth_weight,
    depth_bias,
    norm_gain,
    norm_bias,
    up_weight,
    up_bias,
    down_weight,
    down_bias,
    layer_scale,
    head_gain,
    head_bias,
    embed_store,
    in_weight,
    slide_gain,
    qkv_weight,
    head_slopes,
    tile_coords,
    valid_counts,
):
    n_sec = lax.axis_size("section")
    col_part = in_weight.shape[1] // n_sec
    my_cols = lax.dynamic_slice_in_dim(
        in_weight, lax.axis_index("section") * col_part, col_part, 1
    )
    cols_full = lax.all_gather(my_cols, "slide", axis=0, tiled=True)

    tile_data = tile_features[0].astype(jnp.float32)
    fresh_count = tile_data.shape[0]
    n_rep = lax.axis_size("rep")
    my_rep = lax.axis_index("rep")
    n_slide = lax.axis_size("slide")
    my_slide = lax.axis_index("slide")
    normed = dw_ln(tile_features[0], depth_weight, depth_bias, norm_gain, norm_bias)

    def block_sums(rows):
        hidden = jax.nn.gelu(
            jnp.dot(rows, up_weight, preferred_element_type=jnp.float32) + up_bias,
            approximate=False,
        ).astype(jnp.bfloat16)
        part = jnp.dot(hidden, down_weight, preferred_element_type=jnp.float32).astype(
            jnp.bfloat16
        )
        return jnp.sum(part.astype(jnp.float32).reshape(tile_data.shape), axis=1)

    received = [
        lax.ppermute(normed, "rep", perm=[(r, (r + k) % n_rep) for r in range(n_rep)])
        for k in range(1, n_rep)
    ]
    positions = tile_data.shape[1]
    own_term = jnp.mean(tile_data, axis=1) + layer_scale * (
        block_sums(normed) / positions + down_bias
    )
    peer_terms = [layer_scale * (block_sums(rows) / positions) for rows in received]
    returned = [
        lax.ppermute(term, "rep", perm=[(r, (r - k) % n_rep) for r in range(n_rep)])
        for k, term in enumerate(peer_terms, start=1)
    ]
    pooled = own_term
    for term in returned:
        pooled = pooled + term
    embedded = layer_norm(pooled, head_gain, head_bias, 1e-06).astype(jnp.bfloat16)
    cols_full, embedded = lax.optimization_barrier((cols_full, embedded))
    other_cols = lax.ppermute(
        cols_full, "section", perm=[(c, (c + 1) % n_sec) for c in range(n_sec)]
    )
    first = lax.axis_index("section") == 0
    weight_parts = (cols_full, other_cols, first)

    seq_rows = jnp.concatenate([embedded, embed_store[0, fresh_count:]], axis=0)
    normed_seq = project(seq_rows, weight_parts, slide_gain)
    normed_all = lax.all_gather(normed_seq, "slide", axis=0, tiled=True)
    local_heads = normalize_heads(
        jnp.dot(normed_all, qkv_weight, preferred_element_type=jnp.float32)
    )
    seq_len = local_heads.shape[0]

    heads_here = local_heads.shape[1] // (3 * HDIM)
    arranged = local_heads.reshape(seq_len, heads_here, 3, HDIM)
    queries = arranged[:, :, 0]
    key_rows = arranged[:, :, 1]
    value_rows = arranged[:, :, 2]
    my_slopes = lax.dynamic_slice_in_dim(
        head_slopes, lax.axis_index("slide") * heads_here, heads_here, 0
    )
    coord_x = tile_coords[0, 0].astype(jnp.float32)
    coord_y = tile_coords[0, 1].astype(jnp.float32)
    valid = valid_counts[0]
    key_ok = jnp.arange(seq_len, dtype=jnp.int32) < valid
    inv_root = 1.0 / math.sqrt(HDIM)

    distance = jnp.abs(coord_x[:, None] - coord_x[None, :]) + jnp.abs(
        coord_y[:, None] - coord_y[None, :]
    )
    scores = (
        jnp.einsum("qhd,khd->hqk", queries, key_rows, preferred_element_type=jnp.float32)
        * inv_root
        - my_slopes[:, None, None] * distance[None]
    )
    weights = jnp.where(key_ok[None, None, :], jnp.exp(scores), 0.0).astype(jnp.bfloat16)
    totals = jnp.sum(weights, axis=-1, dtype=jnp.float32)
    weighted = jnp.einsum("hqk,khd->qhd", weights, value_rows, preferred_element_type=jnp.float32)
    safe = jnp.where(key_ok[None, :], totals, 1.0)
    attended = jnp.where(key_ok[:, None, None], weighted / safe.T[:, :, None], 0.0)
    attended = attended.astype(jnp.bfloat16).reshape(seq_len, heads_here * HDIM)
    block = seq_len // n_slide
    pieces = [lax.dynamic_slice_in_dim(attended, my_slide * block, block, 0)]
    for k in range(1, n_slide):
        target = (my_slide + k) % n_slide
        pieces.append(
            lax.ppermute(
                lax.dynamic_slice_in_dim(attended, target * block, block, 0),
                "slide",
                perm=[(j, (j + k) % n_slide) for j in range(n_slide)],
            )
        )
    columns = []
    for group in range(n_slide):
        shift = (my_slide - group) % n_slide
        chosen = pieces[0]
        for k in range(1, n_slide):
            chosen = jnp.where(shift == k, pieces[k], chosen)
        columns.append(chosen)
    context = jnp.concatenate(columns, axis=1)
    return (embedded[None], context[None])


def solution(mesh):
    in_specs = (
        P(("groups", "rep", "section"), "slide", None, None),
        P(),
        P(),
        P(),
        P(),
        P(None, "rep"),
        P("rep"),
        P("rep", None),
        P(),
        P(),
        P(),
        P(),
        P(("groups", "rep", "section"), "slide", None),
        P("slide", None),
        P(),
        P(None, "slide"),
        P(),
        P(("groups", "rep", "section"), None, None),
        P(("groups", "rep", "section")),
    )
    out_specs = (
        P(("groups", "rep", "section"), "slide", None),
        P(("groups", "rep", "section"), "slide", None),
    )
    return jax.shard_map(
        on_device, mesh=mesh, in_specs=in_specs, out_specs=out_specs, check_vma=False
    )
```

```python
import math

import jax
import jax.numpy as jnp
from jax import lax
from jax.experimental import pallas as pl
from jax.experimental.pallas import tpu as pltpu
from jax.sharding import PartitionSpec as P

SIDE = 7
KER = 7
HDIM = 64
LANES = 128


def layer_norm(inputs, gain, shift, epsilon):
    center = jnp.mean(inputs, axis=-1, keepdims=True)
    centered = inputs - center
    spread = jnp.mean(centered * centered, axis=-1, keepdims=True)
    return centered * lax.rsqrt(spread + epsilon) * gain + shift


def dw_ln_kernel(x_ref, w_ref, b_ref, g_ref, nb_ref, o_ref, conv_ref):
    C = x_ref.shape[-1]
    jrow = lax.broadcasted_iota(jnp.int32, (8, LANES), 0)
    masks = [((jrow + (bb - 3)) >= 0) & ((jrow + (bb - 3)) < SIDE) for bb in range(KER)]
    def chunk(ci, carry):
        c0 = pl.multiple_of(ci * LANES, LANES)
        rows = [x_ref[0, i, :, pl.ds(c0, LANES)].astype(jnp.float32) for i in range(SIDE)]
        bias = jnp.broadcast_to(b_ref[:, pl.ds(c0, LANES)], (8, LANES))
        acc = [bias for _ in range(SIDE)]
        for ip in range(SIDE):
            for bb in range(KER):
                s = bb - 3
                sh = rows[ip] if s == 0 else pltpu.roll(rows[ip], shift=(-s) % 8, axis=0)
                sh = jnp.where(masks[bb], sh, 0.0)
                for a in range(KER):
                    i = ip - (a - 3)
                    if 0 <= i < SIDE:
                        wv = jnp.broadcast_to(w_ref[pl.ds(a * KER + bb, 1), pl.ds(c0, LANES)], (8, LANES))
                        acc[i] = acc[i] + sh * wv
        for i in range(SIDE):
            conv_ref[i, :, pl.ds(c0, LANES)] = acc[i]
        return carry
    lax.fori_loop(0, C // LANES, chunk, 0)
    g = g_ref[...]
    nb = nb_ref[...]
    for i in range(SIDE):
        v = conv_ref[i]
        mean = jnp.mean(v, axis=-1, keepdims=True)
        cen = v - mean
        var = jnp.mean(cen * cen, axis=-1, keepdims=True)
        o_ref[0, i] = (cen * lax.rsqrt(var + 1e-06) * g + nb).astype(o_ref.dtype)

def dw_ln(tiles, depth_weight, depth_bias, norm_gain, norm_bias):
    T, _, C = tiles.shape
    x = jnp.pad(tiles.reshape(T, SIDE, SIDE, C), ((0, 0), (0, 0), (0, 1), (0, 0)))
    out = pl.pallas_call(
        dw_ln_kernel,
        grid=(T,),
        in_specs=[
            pl.BlockSpec((1, SIDE, 8, C), lambda t: (t, 0, 0, 0)),
            pl.BlockSpec((KER * KER, C), lambda t: (0, 0)),
            pl.BlockSpec((1, C), lambda t: (0, 0)),
            pl.BlockSpec((1, C), lambda t: (0, 0)),
            pl.BlockSpec((1, C), lambda t: (0, 0)),
        ],
        out_specs=pl.BlockSpec((1, SIDE, 8, C), lambda t: (t, 0, 0, 0)),
        out_shape=jax.ShapeDtypeStruct((T, SIDE, 8, C), jnp.bfloat16),
        scratch_shapes=[pltpu.VMEM((SIDE, 8, C), jnp.float32)],
    )(x, depth_weight, depth_bias[None], norm_gain[None], norm_bias[None])
    return out[:, :, :SIDE].reshape(T * SIDE * SIDE, C)


def normalize_heads(values):
    lead = values.shape[:-1]
    grouped = values.reshape(lead + (-1, 3, HDIM))
    paired = grouped[..., :2, :]
    scaled = paired * lax.rsqrt(jnp.mean(paired * paired, axis=-1, keepdims=True) + 1e-06)
    joined = jnp.concatenate([scaled, grouped[..., 2:, :]], axis=-2)
    return joined.astype(jnp.bfloat16).reshape(lead + (-1,))


def project(rows, weight_parts, slide_gain):
    mine, other, first = weight_parts
    mine_part = jnp.dot(rows, mine, preferred_element_type=jnp.float32)
    other_part = jnp.dot(rows, other, preferred_element_type=jnp.float32)
    projected = jnp.where(
        first,
        jnp.concatenate([mine_part, other_part], axis=-1),
        jnp.concatenate([other_part, mine_part], axis=-1),
    )
    return layer_norm(projected, slide_gain, 0.0, 1e-05).astype(jnp.bfloat16)


def on_device(
    tile_features,
    depth_weight,
    depth_bias,
    norm_gain,
    norm_bias,
    up_weight,
    up_bias,
    down_weight,
    down_bias,
    layer_scale,
    head_gain,
    head_bias,
    embed_store,
    in_weight,
    slide_gain,
    qkv_weight,
    head_slopes,
    tile_coords,
    valid_counts,
):
    n_sec = lax.axis_size("section")
    col_part = in_weight.shape[1] // n_sec
    my_cols = lax.dynamic_slice_in_dim(
        in_weight, lax.axis_index("section") * col_part, col_part, 1
    )
    my_cols, tile_features = lax.optimization_barrier((my_cols, tile_features))
    cols_full = lax.all_gather(my_cols, "slide", axis=0, tiled=True)

    tile_data = tile_features[0].astype(jnp.float32)
    fresh_count = tile_data.shape[0]
    n_rep = lax.axis_size("rep")
    my_rep = lax.axis_index("rep")
    n_slide = lax.axis_size("slide")
    my_slide = lax.axis_index("slide")
    normed = dw_ln(tile_features[0], depth_weight, depth_bias, norm_gain, norm_bias)

    def block_sums(rows):
        hidden = jax.nn.gelu(
            jnp.dot(rows, up_weight, preferred_element_type=jnp.float32) + up_bias,
            approximate=False,
        ).astype(jnp.bfloat16)
        part = jnp.dot(hidden, down_weight, preferred_element_type=jnp.float32).astype(
            jnp.bfloat16
        )
        return jnp.sum(part.astype(jnp.float32).reshape(tile_data.shape), axis=1)

    received = [
        lax.ppermute(normed, "rep", perm=[(r, (r + k) % n_rep) for r in range(n_rep)])
        for k in range(1, n_rep)
    ]
    positions = tile_data.shape[1]
    own_term = jnp.mean(tile_data, axis=1) + layer_scale * (
        block_sums(normed) / positions + down_bias
    )
    peer_terms = [layer_scale * (block_sums(rows) / positions) for rows in received]
    returned = [
        lax.ppermute(term, "rep", perm=[(r, (r - k) % n_rep) for r in range(n_rep)])
        for k, term in enumerate(peer_terms, start=1)
    ]
    pooled = own_term
    for term in returned:
        pooled = pooled + term
    embedded = layer_norm(pooled, head_gain, head_bias, 1e-06).astype(jnp.bfloat16)
    cols_full, embedded = lax.optimization_barrier((cols_full, embedded))
    other_cols = lax.ppermute(
        cols_full, "section", perm=[(c, (c + 1) % n_sec) for c in range(n_sec)]
    )
    first = lax.axis_index("section") == 0
    weight_parts = (cols_full, other_cols, first)

    seq_rows = jnp.concatenate([embedded, embed_store[0, fresh_count:]], axis=0)
    normed_seq = project(seq_rows, weight_parts, slide_gain)
    normed_all = lax.all_gather(normed_seq, "slide", axis=0, tiled=True)
    local_heads = normalize_heads(
        jnp.dot(normed_all, qkv_weight, preferred_element_type=jnp.float32)
    )
    seq_len = local_heads.shape[0]

    heads_here = local_heads.shape[1] // (3 * HDIM)
    arranged = local_heads.reshape(seq_len, heads_here, 3, HDIM)
    queries = arranged[:, :, 0]
    key_rows = arranged[:, :, 1]
    value_rows = arranged[:, :, 2]
    my_slopes = lax.dynamic_slice_in_dim(
        head_slopes, lax.axis_index("slide") * heads_here, heads_here, 0
    )
    coord_x = tile_coords[0, 0].astype(jnp.float32)
    coord_y = tile_coords[0, 1].astype(jnp.float32)
    valid = valid_counts[0]
    key_ok = jnp.arange(seq_len, dtype=jnp.int32) < valid
    inv_root = 1.0 / math.sqrt(HDIM)

    distance = jnp.abs(coord_x[:, None] - coord_x[None, :]) + jnp.abs(
        coord_y[:, None] - coord_y[None, :]
    )
    scores = (
        jnp.einsum("qhd,khd->hqk", queries, key_rows, preferred_element_type=jnp.float32)
        * inv_root
        - my_slopes[:, None, None] * distance[None]
    )
    weights = jnp.where(key_ok[None, None, :], jnp.exp(scores), 0.0).astype(jnp.bfloat16)
    totals = jnp.sum(weights, axis=-1, dtype=jnp.float32)
    weighted = jnp.einsum("hqk,khd->qhd", weights, value_rows, preferred_element_type=jnp.float32)
    safe = jnp.where(key_ok[None, :], totals, 1.0)
    attended = jnp.where(key_ok[:, None, None], weighted / safe.T[:, :, None], 0.0)
    attended = attended.astype(jnp.bfloat16).reshape(seq_len, heads_here * HDIM)
    block = seq_len // n_slide
    pieces = [lax.dynamic_slice_in_dim(attended, my_slide * block, block, 0)]
    for k in range(1, n_slide):
        target = (my_slide + k) % n_slide
        pieces.append(
            lax.ppermute(
                lax.dynamic_slice_in_dim(attended, target * block, block, 0),
                "slide",
                perm=[(j, (j + k) % n_slide) for j in range(n_slide)],
            )
        )
    columns = []
    for group in range(n_slide):
        shift = (my_slide - group) % n_slide
        chosen = pieces[0]
        for k in range(1, n_slide):
            chosen = jnp.where(shift == k, pieces[k], chosen)
        columns.append(chosen)
    context = jnp.concatenate(columns, axis=1)
    return (embedded[None], context[None])


def solution(mesh):
    in_specs = (
        P(("groups", "rep", "section"), "slide", None, None),
        P(),
        P(),
        P(),
        P(),
        P(None, "rep"),
        P("rep"),
        P("rep", None),
        P(),
        P(),
        P(),
        P(),
        P(("groups", "rep", "section"), "slide", None),
        P("slide", None),
        P(),
        P(None, "slide"),
        P(),
        P(("groups", "rep", "section"), None, None),
        P(("groups", "rep", "section")),
    )
    out_specs = (
        P(("groups", "rep", "section"), "slide", None),
        P(("groups", "rep", "section"), "slide", None),
    )
    return jax.shard_map(
        on_device, mesh=mesh, in_specs=in_specs, out_specs=out_specs, check_vma=False
    )
```

```python
import math

import jax
import jax.numpy as jnp
from jax import lax
from jax.experimental import pallas as pl
from jax.experimental.pallas import tpu as pltpu
from jax.sharding import PartitionSpec as P

SIDE = 7
KER = 7
HDIM = 64
LANES = 128


def layer_norm(inputs, gain, shift, epsilon):
    center = jnp.mean(inputs, axis=-1, keepdims=True)
    centered = inputs - center
    spread = jnp.mean(centered * centered, axis=-1, keepdims=True)
    return centered * lax.rsqrt(spread + epsilon) * gain + shift


def dw_ln_kernel(x_ref, w_ref, o_ref, conv_ref):
    C = x_ref.shape[-1]
    jrow = lax.broadcasted_iota(jnp.int32, (8, LANES), 0)
    masks = [((jrow + (bb - 3)) >= 0) & ((jrow + (bb - 3)) < SIDE) for bb in range(KER)]
    def chunk(ci, carry):
        c0 = pl.multiple_of(ci * LANES, LANES)
        rows = [x_ref[0, i, :, pl.ds(c0, LANES)].astype(jnp.float32) for i in range(SIDE)]
        bias = jnp.broadcast_to(w_ref[pl.ds(KER * KER, 1), pl.ds(c0, LANES)], (8, LANES))
        acc = [bias for _ in range(SIDE)]
        for ip in range(SIDE):
            for bb in range(KER):
                s = bb - 3
                sh = rows[ip] if s == 0 else pltpu.roll(rows[ip], shift=(-s) % 8, axis=0)
                sh = jnp.where(masks[bb], sh, 0.0)
                for a in range(KER):
                    i = ip - (a - 3)
                    if 0 <= i < SIDE:
                        wv = jnp.broadcast_to(w_ref[pl.ds(a * KER + bb, 1), pl.ds(c0, LANES)], (8, LANES))
                        acc[i] = acc[i] + sh * wv
        for i in range(SIDE):
            conv_ref[i, :, pl.ds(c0, LANES)] = acc[i]
        return carry
    lax.fori_loop(0, C // LANES, chunk, 0)
    g = w_ref[pl.ds(KER * KER + 1, 1), :]
    nb = w_ref[pl.ds(KER * KER + 2, 1), :]
    for i in range(SIDE):
        v = conv_ref[i]
        mean = jnp.mean(v, axis=-1, keepdims=True)
        cen = v - mean
        var = jnp.mean(cen * cen, axis=-1, keepdims=True)
        o_ref[0, i] = (cen * lax.rsqrt(var + 1e-06) * g + nb).astype(o_ref.dtype)

def dw_ln(tiles, depth_weight, depth_bias, norm_gain, norm_bias):
    T, _, C = tiles.shape
    x = jnp.pad(tiles.reshape(T, SIDE, SIDE, C), ((0, 0), (0, 0), (0, 1), (0, 0)))
    out = pl.pallas_call(
        dw_ln_kernel,
        grid=(T,),
        in_specs=[
            pl.BlockSpec((1, SIDE, 8, C), lambda t: (t, 0, 0, 0)),
            pl.BlockSpec((KER * KER + 3, C), lambda t: (0, 0)),
        ],
        out_specs=pl.BlockSpec((1, SIDE, 8, C), lambda t: (t, 0, 0, 0)),
        out_shape=jax.ShapeDtypeStruct((T, SIDE, 8, C), jnp.bfloat16),
        scratch_shapes=[pltpu.VMEM((SIDE, 8, C), jnp.float32)],
    )(x, jnp.concatenate([depth_weight, depth_bias[None], norm_gain[None], norm_bias[None]]))
    return out[:, :, :SIDE].reshape(T * SIDE * SIDE, C)


def normalize_heads(values):
    lead = values.shape[:-1]
    grouped = values.reshape(lead + (-1, 3, HDIM))
    paired = grouped[..., :2, :]
    scaled = paired * lax.rsqrt(jnp.mean(paired * paired, axis=-1, keepdims=True) + 1e-06)
    joined = jnp.concatenate([scaled, grouped[..., 2:, :]], axis=-2)
    return joined.astype(jnp.bfloat16).reshape(lead + (-1,))


def project(rows, partner_rows, cols, slide_gain):
    n_sec = lax.axis_size("section")
    both = jnp.dot(
        jnp.concatenate([rows, partner_rows], axis=0), cols, preferred_element_type=jnp.float32
    )
    count = rows.shape[0]
    mine = both[:count]
    from_partner = lax.ppermute(
        both[count:], "section", perm=[(c, (c + 1) % n_sec) for c in range(n_sec)]
    )
    projected = jnp.where(
        lax.axis_index("section") == 0,
        jnp.concatenate([mine, from_partner], axis=-1),
        jnp.concatenate([from_partner, mine], axis=-1),
    )
    return layer_norm(projected, slide_gain, 0.0, 1e-05).astype(jnp.bfloat16)


def on_device(
    tile_features,
    depth_weight,
    depth_bias,
    norm_gain,
    norm_bias,
    up_weight,
    up_bias,
    down_weight,
    down_bias,
    layer_scale,
    head_gain,
    head_bias,
    embed_store,
    in_weight,
    slide_gain,
    qkv_weight,
    head_slopes,
    tile_coords,
    valid_counts,
):
    n_sec = lax.axis_size("section")
    col_part = in_weight.shape[1] // n_sec
    my_cols = lax.dynamic_slice_in_dim(
        in_weight, lax.axis_index("section") * col_part, col_part, 1
    )
    cols_full = lax.all_gather(my_cols, "slide", axis=0, tiled=True)

    sec_swap = [(c, (c + 1) % n_sec) for c in range(n_sec)]
    fresh_count = tile_features.shape[1]
    partner_stored = lax.ppermute(embed_store[0, fresh_count:], "section", perm=sec_swap)

    tile_data = tile_features[0].astype(jnp.float32)
    fresh_count = tile_data.shape[0]
    n_rep = lax.axis_size("rep")
    my_rep = lax.axis_index("rep")
    n_slide = lax.axis_size("slide")
    my_slide = lax.axis_index("slide")
    normed = dw_ln(tile_features[0], depth_weight, depth_bias, norm_gain, norm_bias)

    def block_sums(rows):
        hidden = jax.nn.gelu(
            jnp.dot(rows, up_weight, preferred_element_type=jnp.float32) + up_bias,
            approximate=False,
        ).astype(jnp.bfloat16)
        part = jnp.dot(hidden, down_weight, preferred_element_type=jnp.float32).astype(
            jnp.bfloat16
        )
        return jnp.sum(part.astype(jnp.float32).reshape(tile_data.shape), axis=1)

    received = [
        lax.ppermute(normed, "rep", perm=[(r, (r + k) % n_rep) for r in range(n_rep)])
        for k in range(1, n_rep)
    ]
    positions = tile_data.shape[1]
    own_term = jnp.mean(tile_data, axis=1) + layer_scale * (
        block_sums(normed) / positions + down_bias
    )
    peer_terms = [layer_scale * (block_sums(rows) / positions) for rows in received]
    returned = [
        lax.ppermute(term, "rep", perm=[(r, (r - k) % n_rep) for r in range(n_rep)])
        for k, term in enumerate(peer_terms, start=1)
    ]
    pooled = own_term
    for term in returned:
        pooled = pooled + term
    embedded = layer_norm(pooled, head_gain, head_bias, 1e-06).astype(jnp.bfloat16)
    cols_full, embedded = lax.optimization_barrier((cols_full, embedded))
    partner_embedded = lax.ppermute(embedded, "section", perm=sec_swap)

    seq_rows = jnp.concatenate([embedded, embed_store[0, fresh_count:]], axis=0)
    partner_rows = jnp.concatenate([partner_embedded, partner_stored], axis=0)
    normed_seq = project(seq_rows, partner_rows, cols_full, slide_gain)
    normed_all = lax.all_gather(normed_seq, "slide", axis=0, tiled=True)
    local_heads = normalize_heads(
        jnp.dot(normed_all, qkv_weight, preferred_element_type=jnp.float32)
    )
    seq_len = local_heads.shape[0]

    heads_here = local_heads.shape[1] // (3 * HDIM)
    arranged = local_heads.reshape(seq_len, heads_here, 3, HDIM)
    queries = arranged[:, :, 0]
    key_rows = arranged[:, :, 1]
    value_rows = arranged[:, :, 2]
    my_slopes = lax.dynamic_slice_in_dim(
        head_slopes, lax.axis_index("slide") * heads_here, heads_here, 0
    )
    coord_x = tile_coords[0, 0].astype(jnp.float32)
    coord_y = tile_coords[0, 1].astype(jnp.float32)
    valid = valid_counts[0]
    key_ok = jnp.arange(seq_len, dtype=jnp.int32) < valid
    inv_root = 1.0 / math.sqrt(HDIM)

    distance = jnp.abs(coord_x[:, None] - coord_x[None, :]) + jnp.abs(
        coord_y[:, None] - coord_y[None, :]
    )
    scores = (
        jnp.einsum("qhd,khd->hqk", queries, key_rows, preferred_element_type=jnp.float32)
        * inv_root
        - my_slopes[:, None, None] * distance[None]
    )
    weights = jnp.where(key_ok[None, None, :], jnp.exp(scores), 0.0).astype(jnp.bfloat16)
    totals = jnp.sum(weights, axis=-1, dtype=jnp.float32)
    weighted = jnp.einsum("hqk,khd->qhd", weights, value_rows, preferred_element_type=jnp.float32)
    safe = jnp.where(key_ok[None, :], totals, 1.0)
    attended = jnp.where(key_ok[:, None, None], weighted / safe.T[:, :, None], 0.0)
    attended = attended.astype(jnp.bfloat16).reshape(seq_len, heads_here * HDIM)
    context = lax.all_to_all(attended, "slide", split_axis=0, concat_axis=1, tiled=True)
    return (embedded[None], context[None])


def solution(mesh):
    in_specs = (
        P(("groups", "rep", "section"), "slide", None, None),
        P(),
        P(),
        P(),
        P(),
        P(None, "rep"),
        P("rep"),
        P("rep", None),
        P(),
        P(),
        P(),
        P(),
        P(("groups", "rep", "section"), "slide", None),
        P("slide", None),
        P(),
        P(None, "slide"),
        P(),
        P(("groups", "rep", "section"), None, None),
        P(("groups", "rep", "section")),
    )
    out_specs = (
        P(("groups", "rep", "section"), "slide", None),
        P(("groups", "rep", "section"), "slide", None),
    )
    return jax.shard_map(
        on_device, mesh=mesh, in_specs=in_specs, out_specs=out_specs, check_vma=False
    )
```

```python
import math

import jax
import jax.numpy as jnp
from jax import lax
from jax.experimental import pallas as pl
from jax.experimental.pallas import tpu as pltpu
from jax.sharding import PartitionSpec as P

SIDE = 7
KER = 7
HDIM = 64
LANES = 128


def layer_norm(inputs, gain, shift, epsilon):
    center = jnp.mean(inputs, axis=-1, keepdims=True)
    centered = inputs - center
    spread = jnp.mean(centered * centered, axis=-1, keepdims=True)
    return centered * lax.rsqrt(spread + epsilon) * gain + shift


def dw_ln_kernel(x_ref, w_ref, o_ref, conv_ref):
    C = x_ref.shape[-1]
    jrow = lax.broadcasted_iota(jnp.int32, (8, LANES), 0)
    masks = [((jrow + (bb - 3)) >= 0) & ((jrow + (bb - 3)) < SIDE) for bb in range(KER)]
    def chunk(ci, carry):
        c0 = pl.multiple_of(ci * LANES, LANES)
        rows = [x_ref[0, i, :, pl.ds(c0, LANES)].astype(jnp.float32) for i in range(SIDE)]
        bias = jnp.broadcast_to(w_ref[pl.ds(KER * KER, 1), pl.ds(c0, LANES)], (8, LANES))
        acc = [bias for _ in range(SIDE)]
        for ip in range(SIDE):
            for bb in range(KER):
                s = bb - 3
                sh = rows[ip] if s == 0 else pltpu.roll(rows[ip], shift=(-s) % 8, axis=0)
                sh = jnp.where(masks[bb], sh, 0.0)
                for a in range(KER):
                    i = ip - (a - 3)
                    if 0 <= i < SIDE:
                        wv = jnp.broadcast_to(w_ref[pl.ds(a * KER + bb, 1), pl.ds(c0, LANES)], (8, LANES))
                        acc[i] = acc[i] + sh * wv
        for i in range(SIDE):
            conv_ref[i, :, pl.ds(c0, LANES)] = acc[i]
        return carry
    lax.fori_loop(0, C // LANES, chunk, 0)
    g = w_ref[pl.ds(KER * KER + 1, 1), :]
    nb = w_ref[pl.ds(KER * KER + 2, 1), :]
    for i in range(SIDE):
        v = conv_ref[i]
        mean = jnp.mean(v, axis=-1, keepdims=True)
        cen = v - mean
        var = jnp.mean(cen * cen, axis=-1, keepdims=True)
        o_ref[0, i] = (cen * lax.rsqrt(var + 1e-06) * g + nb).astype(o_ref.dtype)

def dw_ln(tiles, depth_weight, depth_bias, norm_gain, norm_bias):
    T, _, C = tiles.shape
    x = jnp.pad(tiles.reshape(T, SIDE, SIDE, C), ((0, 0), (0, 0), (0, 1), (0, 0)))
    out = pl.pallas_call(
        dw_ln_kernel,
        grid=(T,),
        in_specs=[
            pl.BlockSpec((1, SIDE, 8, C), lambda t: (t, 0, 0, 0)),
            pl.BlockSpec((KER * KER + 3, C), lambda t: (0, 0)),
        ],
        out_specs=pl.BlockSpec((1, SIDE, 8, C), lambda t: (t, 0, 0, 0)),
        out_shape=jax.ShapeDtypeStruct((T, SIDE, 8, C), jnp.bfloat16),
        scratch_shapes=[pltpu.VMEM((SIDE, 8, C), jnp.float32)],
    )(x, jnp.concatenate([depth_weight, depth_bias[None], norm_gain[None], norm_bias[None]]))
    return out[:, :, :SIDE].reshape(T * SIDE * SIDE, C)


def normalize_heads(values):
    lead = values.shape[:-1]
    grouped = values.reshape(lead + (-1, 3, HDIM))
    paired = grouped[..., :2, :]
    scaled = paired * lax.rsqrt(jnp.mean(paired * paired, axis=-1, keepdims=True) + 1e-06)
    joined = jnp.concatenate([scaled, grouped[..., 2:, :]], axis=-2)
    return joined.astype(jnp.bfloat16).reshape(lead + (-1,))


def project(rows, partner_rows, cols, slide_gain):
    n_sec = lax.axis_size("section")
    joined = jnp.concatenate([rows, partner_rows], axis=0)
    n_blocks, n_grp, block_rows, _ = cols.shape
    both = jnp.einsum(
        "njk,jgkc->ngc",
        joined.reshape(joined.shape[0], n_blocks, block_rows),
        cols,
        preferred_element_type=jnp.float32,
    ).reshape(joined.shape[0], -1)
    count = rows.shape[0]
    mine = both[:count]
    from_partner = lax.ppermute(
        both[count:], "section", perm=[(c, (c + 1) % n_sec) for c in range(n_sec)]
    )
    projected = jnp.where(
        lax.axis_index("section") == 0,
        jnp.concatenate([mine, from_partner], axis=-1),
        jnp.concatenate([from_partner, mine], axis=-1),
    )
    return layer_norm(projected, slide_gain, 0.0, 1e-05).astype(jnp.bfloat16)


def on_device(
    tile_features,
    depth_weight,
    depth_bias,
    norm_gain,
    norm_bias,
    up_weight,
    up_bias,
    down_weight,
    down_bias,
    layer_scale,
    head_gain,
    head_bias,
    embed_store,
    in_weight,
    slide_gain,
    qkv_weight,
    head_slopes,
    tile_coords,
    valid_counts,
):
    n_sec = lax.axis_size("section")
    col_part = in_weight.shape[1] // n_sec
    n_grp = lax.axis_size("groups")
    sub_part = col_part // n_grp
    my_cols = lax.dynamic_slice_in_dim(
        in_weight,
        lax.axis_index("section") * col_part + lax.axis_index("groups") * sub_part,
        sub_part,
        1,
    )
    cols_full = lax.all_gather(my_cols, ("slide", "groups"), axis=0, tiled=False)
    cols_full = cols_full.reshape((-1, n_grp) + my_cols.shape)

    sec_swap = [(c, (c + 1) % n_sec) for c in range(n_sec)]
    fresh_count = tile_features.shape[1]
    partner_stored = lax.ppermute(embed_store[0, fresh_count:], "section", perm=sec_swap)

    tile_data = tile_features[0].astype(jnp.float32)
    fresh_count = tile_data.shape[0]
    n_rep = lax.axis_size("rep")
    my_rep = lax.axis_index("rep")
    n_slide = lax.axis_size("slide")
    my_slide = lax.axis_index("slide")
    normed = dw_ln(tile_features[0], depth_weight, depth_bias, norm_gain, norm_bias)

    def block_sums(rows):
        hidden = jax.nn.gelu(
            jnp.dot(rows, up_weight, preferred_element_type=jnp.float32) + up_bias,
            approximate=False,
        ).astype(jnp.bfloat16)
        part = jnp.dot(hidden, down_weight, preferred_element_type=jnp.float32).astype(
            jnp.bfloat16
        )
        return jnp.sum(part.astype(jnp.float32).reshape(tile_data.shape), axis=1)

    received = [
        lax.ppermute(normed, "rep", perm=[(r, (r + k) % n_rep) for r in range(n_rep)])
        for k in range(1, n_rep)
    ]
    positions = tile_data.shape[1]
    own_term = jnp.mean(tile_data, axis=1) + layer_scale * (
        block_sums(normed) / positions + down_bias
    )
    peer_terms = [layer_scale * (block_sums(rows) / positions) for rows in received]
    returned = [
        lax.ppermute(term, "rep", perm=[(r, (r - k) % n_rep) for r in range(n_rep)])
        for k, term in enumerate(peer_terms, start=1)
    ]
    pooled = own_term
    for term in returned:
        pooled = pooled + term
    embedded = layer_norm(pooled, head_gain, head_bias, 1e-06).astype(jnp.bfloat16)
    cols_full, embedded = lax.optimization_barrier((cols_full, embedded))
    partner_embedded = lax.ppermute(embedded, "section", perm=sec_swap)

    seq_rows = jnp.concatenate([embedded, embed_store[0, fresh_count:]], axis=0)
    partner_rows = jnp.concatenate([partner_embedded, partner_stored], axis=0)
    normed_seq = project(seq_rows, partner_rows, cols_full, slide_gain)
    normed_all = lax.all_gather(normed_seq, "slide", axis=0, tiled=True)
    local_heads = normalize_heads(
        jnp.dot(normed_all, qkv_weight, preferred_element_type=jnp.float32)
    )
    seq_len = local_heads.shape[0]

    heads_here = local_heads.shape[1] // (3 * HDIM)
    arranged = local_heads.reshape(seq_len, heads_here, 3, HDIM)
    queries = arranged[:, :, 0]
    key_rows = arranged[:, :, 1]
    value_rows = arranged[:, :, 2]
    my_slopes = lax.dynamic_slice_in_dim(
        head_slopes, lax.axis_index("slide") * heads_here, heads_here, 0
    )
    coord_x = tile_coords[0, 0].astype(jnp.float32)
    coord_y = tile_coords[0, 1].astype(jnp.float32)
    valid = valid_counts[0]
    key_ok = jnp.arange(seq_len, dtype=jnp.int32) < valid
    inv_root = 1.0 / math.sqrt(HDIM)

    distance = jnp.abs(coord_x[:, None] - coord_x[None, :]) + jnp.abs(
        coord_y[:, None] - coord_y[None, :]
    )
    scores = (
        jnp.einsum("qhd,khd->hqk", queries, key_rows, preferred_element_type=jnp.float32)
        * inv_root
        - my_slopes[:, None, None] * distance[None]
    )
    weights = jnp.where(key_ok[None, None, :], jnp.exp(scores), 0.0).astype(jnp.bfloat16)
    totals = jnp.sum(weights, axis=-1, dtype=jnp.float32)
    weighted = jnp.einsum("hqk,khd->qhd", weights, value_rows, preferred_element_type=jnp.float32)
    safe = jnp.where(key_ok[None, :], totals, 1.0)
    attended = jnp.where(key_ok[:, None, None], weighted / safe.T[:, :, None], 0.0)
    attended = attended.astype(jnp.bfloat16).reshape(seq_len, heads_here * HDIM)
    context = lax.all_to_all(attended, "slide", split_axis=0, concat_axis=1, tiled=True)
    return (embedded[None], context[None])


def solution(mesh):
    in_specs = (
        P(("groups", "rep", "section"), "slide", None, None),
        P(),
        P(),
        P(),
        P(),
        P(None, "rep"),
        P("rep"),
        P("rep", None),
        P(),
        P(),
        P(),
        P(),
        P(("groups", "rep", "section"), "slide", None),
        P("slide", None),
        P(),
        P(None, "slide"),
        P(),
        P(("groups", "rep", "section"), None, None),
        P(("groups", "rep", "section")),
    )
    out_specs = (
        P(("groups", "rep", "section"), "slide", None),
        P(("groups", "rep", "section"), "slide", None),
    )
    return jax.shard_map(
        on_device, mesh=mesh, in_specs=in_specs, out_specs=out_specs, check_vma=False
    )
```

```python
import math

import jax
import jax.numpy as jnp
from jax import lax
from jax.experimental import pallas as pl
from jax.experimental.pallas import tpu as pltpu
from jax.sharding import PartitionSpec as P

SIDE = 7
KER = 7
HDIM = 64
LANES = 128


def layer_norm(inputs, gain, shift, epsilon):
    center = jnp.mean(inputs, axis=-1, keepdims=True)
    centered = inputs - center
    spread = jnp.mean(centered * centered, axis=-1, keepdims=True)
    return centered * lax.rsqrt(spread + epsilon) * gain + shift


def dw_ln_kernel(x_ref, w_ref, o_ref, conv_ref):
    C = x_ref.shape[-1]
    jrow = lax.broadcasted_iota(jnp.int32, (8, LANES), 0)
    masks = [((jrow + (bb - 3)) >= 0) & ((jrow + (bb - 3)) < SIDE) for bb in range(KER)]
    def chunk(ci, carry):
        c0 = pl.multiple_of(ci * LANES, LANES)
        rows = [x_ref[0, i, :, pl.ds(c0, LANES)].astype(jnp.float32) for i in range(SIDE)]
        bias = jnp.broadcast_to(w_ref[pl.ds(KER * KER, 1), pl.ds(c0, LANES)], (8, LANES))
        acc = [bias for _ in range(SIDE)]
        for ip in range(SIDE):
            for bb in range(KER):
                s = bb - 3
                sh = rows[ip] if s == 0 else pltpu.roll(rows[ip], shift=(-s) % 8, axis=0)
                sh = jnp.where(masks[bb], sh, 0.0)
                for a in range(KER):
                    i = ip - (a - 3)
                    if 0 <= i < SIDE:
                        wv = jnp.broadcast_to(w_ref[pl.ds(a * KER + bb, 1), pl.ds(c0, LANES)], (8, LANES))
                        acc[i] = acc[i] + sh * wv
        for i in range(SIDE):
            conv_ref[i, :, pl.ds(c0, LANES)] = acc[i]
        return carry
    lax.fori_loop(0, C // LANES, chunk, 0)
    g = w_ref[pl.ds(KER * KER + 1, 1), :]
    nb = w_ref[pl.ds(KER * KER + 2, 1), :]
    for i in range(SIDE):
        v = conv_ref[i]
        mean = jnp.mean(v, axis=-1, keepdims=True)
        cen = v - mean
        var = jnp.mean(cen * cen, axis=-1, keepdims=True)
        o_ref[0, i] = (cen * lax.rsqrt(var + 1e-06) * g + nb).astype(o_ref.dtype)

def dw_ln(tiles, depth_weight, depth_bias, norm_gain, norm_bias):
    T, _, C = tiles.shape
    x = jnp.pad(tiles.reshape(T, SIDE, SIDE, C), ((0, 0), (0, 0), (0, 1), (0, 0)))
    out = pl.pallas_call(
        dw_ln_kernel,
        grid=(T,),
        in_specs=[
            pl.BlockSpec((1, SIDE, 8, C), lambda t: (t, 0, 0, 0)),
            pl.BlockSpec((KER * KER + 3, C), lambda t: (0, 0)),
        ],
        out_specs=pl.BlockSpec((1, SIDE, 8, C), lambda t: (t, 0, 0, 0)),
        out_shape=jax.ShapeDtypeStruct((T, SIDE, 8, C), jnp.bfloat16),
        scratch_shapes=[pltpu.VMEM((SIDE, 8, C), jnp.float32)],
    )(x, jnp.concatenate([depth_weight, depth_bias[None], norm_gain[None], norm_bias[None]]))
    return out[:, :, :SIDE].reshape(T * SIDE * SIDE, C)


def normalize_heads(values):
    lead = values.shape[:-1]
    grouped = values.reshape(lead + (-1, 3, HDIM))
    paired = grouped[..., :2, :]
    scaled = paired * lax.rsqrt(jnp.mean(paired * paired, axis=-1, keepdims=True) + 1e-06)
    joined = jnp.concatenate([scaled, grouped[..., 2:, :]], axis=-2)
    return joined.astype(jnp.bfloat16).reshape(lead + (-1,))


def project(rows, partner_rows, cols, slide_gain):
    n_sec = lax.axis_size("section")
    both = jnp.dot(
        jnp.concatenate([rows, partner_rows], axis=0), cols, preferred_element_type=jnp.float32
    )
    count = rows.shape[0]
    mine = both[:count]
    from_partner = lax.ppermute(
        both[count:], "section", perm=[(c, (c + 1) % n_sec) for c in range(n_sec)]
    )
    projected = jnp.where(
        lax.axis_index("section") == 0,
        jnp.concatenate([mine, from_partner], axis=-1),
        jnp.concatenate([from_partner, mine], axis=-1),
    )
    return layer_norm(projected, slide_gain, 0.0, 1e-05).astype(jnp.bfloat16)


def on_device(
    tile_features,
    depth_weight,
    depth_bias,
    norm_gain,
    norm_bias,
    up_weight,
    up_bias,
    down_weight,
    down_bias,
    layer_scale,
    head_gain,
    head_bias,
    embed_store,
    in_weight,
    slide_gain,
    qkv_weight,
    head_slopes,
    tile_coords,
    valid_counts,
):
    n_sec = lax.axis_size("section")
    col_part = in_weight.shape[1] // n_sec
    my_cols = lax.dynamic_slice_in_dim(
        in_weight, lax.axis_index("section") * col_part, col_part, 1
    )
    cols_full = lax.all_gather(my_cols, "slide", axis=0, tiled=True)

    sec_swap = [(c, (c + 1) % n_sec) for c in range(n_sec)]
    fresh_count = tile_features.shape[1]
    partner_stored = lax.ppermute(embed_store[0, fresh_count:], "section", perm=sec_swap)

    tile_data = tile_features[0].astype(jnp.float32)
    fresh_count = tile_data.shape[0]
    n_rep = lax.axis_size("rep")
    my_rep = lax.axis_index("rep")
    n_slide = lax.axis_size("slide")
    my_slide = lax.axis_index("slide")
    normed = dw_ln(tile_features[0], depth_weight, depth_bias, norm_gain, norm_bias)

    def block_sums(rows):
        hidden = jax.nn.gelu(
            jnp.dot(rows, up_weight, preferred_element_type=jnp.float32) + up_bias,
            approximate=False,
        ).astype(jnp.bfloat16)
        part = jnp.dot(hidden, down_weight, preferred_element_type=jnp.float32).astype(
            jnp.bfloat16
        )
        return jnp.sum(part.astype(jnp.float32).reshape(tile_data.shape), axis=1)

    received = [
        lax.ppermute(normed, "rep", perm=[(r, (r + k) % n_rep) for r in range(n_rep)])
        for k in range(1, n_rep)
    ]
    positions = tile_data.shape[1]
    own_term = jnp.mean(tile_data, axis=1) + layer_scale * (
        block_sums(normed) / positions + down_bias
    )
    peer_terms = [layer_scale * (block_sums(rows) / positions) for rows in received]
    returned = [
        lax.ppermute(term, "rep", perm=[(r, (r - k) % n_rep) for r in range(n_rep)])
        for k, term in enumerate(peer_terms, start=1)
    ]
    pooled = own_term
    for term in returned:
        pooled = pooled + term
    embedded = layer_norm(pooled, head_gain, head_bias, 1e-06).astype(jnp.bfloat16)
    partner_embedded = lax.ppermute(embedded, "section", perm=sec_swap)
    cols_full, embedded, partner_embedded = lax.optimization_barrier(
        (cols_full, embedded, partner_embedded)
    )

    seq_rows = jnp.concatenate([embedded, embed_store[0, fresh_count:]], axis=0)
    partner_rows = jnp.concatenate([partner_embedded, partner_stored], axis=0)
    normed_seq = project(seq_rows, partner_rows, cols_full, slide_gain)
    normed_all = lax.all_gather(normed_seq, "slide", axis=0, tiled=True)
    local_heads = normalize_heads(
        jnp.dot(normed_all, qkv_weight, preferred_element_type=jnp.float32)
    )
    seq_len = local_heads.shape[0]

    heads_here = local_heads.shape[1] // (3 * HDIM)
    arranged = local_heads.reshape(seq_len, heads_here, 3, HDIM)
    queries = arranged[:, :, 0]
    key_rows = arranged[:, :, 1]
    value_rows = arranged[:, :, 2]
    my_slopes = lax.dynamic_slice_in_dim(
        head_slopes, lax.axis_index("slide") * heads_here, heads_here, 0
    )
    coord_x = tile_coords[0, 0].astype(jnp.float32)
    coord_y = tile_coords[0, 1].astype(jnp.float32)
    valid = valid_counts[0]
    key_ok = jnp.arange(seq_len, dtype=jnp.int32) < valid
    inv_root = 1.0 / math.sqrt(HDIM)

    distance = jnp.abs(coord_x[:, None] - coord_x[None, :]) + jnp.abs(
        coord_y[:, None] - coord_y[None, :]
    )
    scores = (
        jnp.einsum("qhd,khd->hqk", queries, key_rows, preferred_element_type=jnp.float32)
        * inv_root
        - my_slopes[:, None, None] * distance[None]
    )
    weights = jnp.where(key_ok[None, None, :], jnp.exp(scores), 0.0).astype(jnp.bfloat16)
    totals = jnp.sum(weights, axis=-1, dtype=jnp.float32)
    weighted = jnp.einsum("hqk,khd->qhd", weights, value_rows, preferred_element_type=jnp.float32)
    safe = jnp.where(key_ok[None, :], totals, 1.0)
    attended = jnp.where(key_ok[:, None, None], weighted / safe.T[:, :, None], 0.0)
    attended = attended.astype(jnp.bfloat16).reshape(seq_len, heads_here * HDIM)
    context = lax.all_to_all(attended, "slide", split_axis=0, concat_axis=1, tiled=True)
    return (embedded[None], context[None])


def solution(mesh):
    in_specs = (
        P(("groups", "rep", "section"), "slide", None, None),
        P(),
        P(),
        P(),
        P(),
        P(None, "rep"),
        P("rep"),
        P("rep", None),
        P(),
        P(),
        P(),
        P(),
        P(("groups", "rep", "section"), "slide", None),
        P("slide", None),
        P(),
        P(None, "slide"),
        P(),
        P(("groups", "rep", "section"), None, None),
        P(("groups", "rep", "section")),
    )
    out_specs = (
        P(("groups", "rep", "section"), "slide", None),
        P(("groups", "rep", "section"), "slide", None),
    )
    return jax.shard_map(
        on_device, mesh=mesh, in_specs=in_specs, out_specs=out_specs, check_vma=False
    )
```

```python
import math

import jax
import jax.numpy as jnp
from jax import lax
from jax.experimental import pallas as pl
from jax.experimental.pallas import tpu as pltpu
from jax.sharding import PartitionSpec as P

SIDE = 7
KER = 7
HDIM = 64
LANES = 128


def layer_norm(inputs, gain, shift, epsilon):
    center = jnp.mean(inputs, axis=-1, keepdims=True)
    centered = inputs - center
    spread = jnp.mean(centered * centered, axis=-1, keepdims=True)
    return centered * lax.rsqrt(spread + epsilon) * gain + shift


def dw_ln_kernel(x_ref, w_ref, o_ref, conv_ref):
    C = x_ref.shape[-1]
    jrow = lax.broadcasted_iota(jnp.int32, (8, LANES), 0)
    masks = [((jrow + (bb - 3)) >= 0) & ((jrow + (bb - 3)) < SIDE) for bb in range(KER)]
    def chunk(ci, carry):
        c0 = pl.multiple_of(ci * LANES, LANES)
        rows = [x_ref[0, i, :, pl.ds(c0, LANES)].astype(jnp.float32) for i in range(SIDE)]
        bias = jnp.broadcast_to(w_ref[pl.ds(KER * KER, 1), pl.ds(c0, LANES)], (8, LANES))
        acc = [bias for _ in range(SIDE)]
        for ip in range(SIDE):
            for bb in range(KER):
                s = bb - 3
                sh = rows[ip] if s == 0 else pltpu.roll(rows[ip], shift=(-s) % 8, axis=0)
                sh = jnp.where(masks[bb], sh, 0.0)
                for a in range(KER):
                    i = ip - (a - 3)
                    if 0 <= i < SIDE:
                        wv = jnp.broadcast_to(w_ref[pl.ds(a * KER + bb, 1), pl.ds(c0, LANES)], (8, LANES))
                        acc[i] = acc[i] + sh * wv
        for i in range(SIDE):
            conv_ref[i, :, pl.ds(c0, LANES)] = acc[i]
        return carry
    lax.fori_loop(0, C // LANES, chunk, 0)
    g = w_ref[pl.ds(KER * KER + 1, 1), :]
    nb = w_ref[pl.ds(KER * KER + 2, 1), :]
    for i in range(SIDE):
        v = conv_ref[i]
        mean = jnp.mean(v, axis=-1, keepdims=True)
        cen = v - mean
        var = jnp.mean(cen * cen, axis=-1, keepdims=True)
        o_ref[0, i] = (cen * lax.rsqrt(var + 1e-06) * g + nb).astype(o_ref.dtype)

def dw_ln(tiles, depth_weight, depth_bias, norm_gain, norm_bias):
    T, _, C = tiles.shape
    x = jnp.pad(tiles.reshape(T, SIDE, SIDE, C), ((0, 0), (0, 0), (0, 1), (0, 0)))
    out = pl.pallas_call(
        dw_ln_kernel,
        grid=(T,),
        in_specs=[
            pl.BlockSpec((1, SIDE, 8, C), lambda t: (t, 0, 0, 0)),
            pl.BlockSpec((KER * KER + 3, C), lambda t: (0, 0)),
        ],
        out_specs=pl.BlockSpec((1, SIDE, 8, C), lambda t: (t, 0, 0, 0)),
        out_shape=jax.ShapeDtypeStruct((T, SIDE, 8, C), jnp.bfloat16),
        scratch_shapes=[pltpu.VMEM((SIDE, 8, C), jnp.float32)],
    )(x, jnp.concatenate([depth_weight, depth_bias[None], norm_gain[None], norm_bias[None]]))
    return out[:, :, :SIDE].reshape(T * SIDE * SIDE, C)


def normalize_heads(values):
    lead = values.shape[:-1]
    grouped = values.reshape(lead + (-1, 3, HDIM))
    paired = grouped[..., :2, :]
    scaled = paired * lax.rsqrt(jnp.mean(paired * paired, axis=-1, keepdims=True) + 1e-06)
    joined = jnp.concatenate([scaled, grouped[..., 2:, :]], axis=-2)
    return joined.astype(jnp.bfloat16).reshape(lead + (-1,))


def project(rows, partner_rows, weight_rows, slide_gain):
    n_sec = lax.axis_size("section")
    joined = jnp.concatenate([rows, partner_rows], axis=0)
    n_blocks, part_rows, _ = weight_rows.shape
    picked = lax.dynamic_index_in_dim(
        joined.reshape(joined.shape[0], n_blocks, n_sec, part_rows),
        lax.axis_index("section"),
        2,
        keepdims=False,
    )
    both = jnp.einsum("njk,jkc->nc", picked, weight_rows, preferred_element_type=jnp.float32)
    count = rows.shape[0]
    from_partner = lax.ppermute(
        both[count:], "section", perm=[(c, (c + 1) % n_sec) for c in range(n_sec)]
    )
    projected = both[:count] + from_partner
    return layer_norm(projected, slide_gain, 0.0, 1e-05).astype(jnp.bfloat16)


def on_device(
    tile_features,
    depth_weight,
    depth_bias,
    norm_gain,
    norm_bias,
    up_weight,
    up_bias,
    down_weight,
    down_bias,
    layer_scale,
    head_gain,
    head_bias,
    embed_store,
    in_weight,
    slide_gain,
    qkv_weight,
    head_slopes,
    tile_coords,
    valid_counts,
):
    n_sec = lax.axis_size("section")
    row_part = in_weight.shape[0] // n_sec
    my_rows = lax.dynamic_slice_in_dim(
        in_weight, lax.axis_index("section") * row_part, row_part, 0
    )
    cols_full = lax.all_gather(my_rows, "slide", axis=0, tiled=False)

    sec_swap = [(c, (c + 1) % n_sec) for c in range(n_sec)]
    fresh_count = tile_features.shape[1]
    partner_stored = lax.ppermute(embed_store[0, fresh_count:], "section", perm=sec_swap)

    tile_data = tile_features[0].astype(jnp.float32)
    fresh_count = tile_data.shape[0]
    n_rep = lax.axis_size("rep")
    my_rep = lax.axis_index("rep")
    n_slide = lax.axis_size("slide")
    my_slide = lax.axis_index("slide")
    normed = dw_ln(tile_features[0], depth_weight, depth_bias, norm_gain, norm_bias)

    def block_sums(rows):
        hidden = jax.nn.gelu(
            jnp.dot(rows, up_weight, preferred_element_type=jnp.float32) + up_bias,
            approximate=False,
        ).astype(jnp.bfloat16)
        part = jnp.dot(hidden, down_weight, preferred_element_type=jnp.float32).astype(
            jnp.bfloat16
        )
        return jnp.sum(part.astype(jnp.float32).reshape(tile_data.shape), axis=1)

    received = [
        lax.ppermute(normed, "rep", perm=[(r, (r + k) % n_rep) for r in range(n_rep)])
        for k in range(1, n_rep)
    ]
    positions = tile_data.shape[1]
    own_term = jnp.mean(tile_data, axis=1) + layer_scale * (
        block_sums(normed) / positions + down_bias
    )
    peer_terms = [layer_scale * (block_sums(rows) / positions) for rows in received]
    returned = [
        lax.ppermute(term, "rep", perm=[(r, (r - k) % n_rep) for r in range(n_rep)])
        for k, term in enumerate(peer_terms, start=1)
    ]
    pooled = own_term
    for term in returned:
        pooled = pooled + term
    embedded = layer_norm(pooled, head_gain, head_bias, 1e-06).astype(jnp.bfloat16)
    partner_embedded = lax.ppermute(embedded, "section", perm=sec_swap)
    cols_full, embedded, partner_embedded = lax.optimization_barrier(
        (cols_full, embedded, partner_embedded)
    )

    seq_rows = jnp.concatenate([embedded, embed_store[0, fresh_count:]], axis=0)
    partner_rows = jnp.concatenate([partner_embedded, partner_stored], axis=0)
    normed_seq = project(seq_rows, partner_rows, cols_full, slide_gain)
    normed_all = lax.all_gather(normed_seq, "slide", axis=0, tiled=True)
    local_heads = normalize_heads(
        jnp.dot(normed_all, qkv_weight, preferred_element_type=jnp.float32)
    )
    seq_len = local_heads.shape[0]

    heads_here = local_heads.shape[1] // (3 * HDIM)
    arranged = local_heads.reshape(seq_len, heads_here, 3, HDIM)
    queries = arranged[:, :, 0]
    key_rows = arranged[:, :, 1]
    value_rows = arranged[:, :, 2]
    my_slopes = lax.dynamic_slice_in_dim(
        head_slopes, lax.axis_index("slide") * heads_here, heads_here, 0
    )
    coord_x = tile_coords[0, 0].astype(jnp.float32)
    coord_y = tile_coords[0, 1].astype(jnp.float32)
    valid = valid_counts[0]
    key_ok = jnp.arange(seq_len, dtype=jnp.int32) < valid
    inv_root = 1.0 / math.sqrt(HDIM)

    distance = jnp.abs(coord_x[:, None] - coord_x[None, :]) + jnp.abs(
        coord_y[:, None] - coord_y[None, :]
    )
    scores = (
        jnp.einsum("qhd,khd->hqk", queries, key_rows, preferred_element_type=jnp.float32)
        * inv_root
        - my_slopes[:, None, None] * distance[None]
    )
    weights = jnp.where(key_ok[None, None, :], jnp.exp(scores), 0.0).astype(jnp.bfloat16)
    totals = jnp.sum(weights, axis=-1, dtype=jnp.float32)
    weighted = jnp.einsum("hqk,khd->qhd", weights, value_rows, preferred_element_type=jnp.float32)
    safe = jnp.where(key_ok[None, :], totals, 1.0)
    attended = jnp.where(key_ok[:, None, None], weighted / safe.T[:, :, None], 0.0)
    attended = attended.astype(jnp.bfloat16).reshape(seq_len, heads_here * HDIM)
    context = lax.all_to_all(attended, "slide", split_axis=0, concat_axis=1, tiled=True)
    return (embedded[None], context[None])


def solution(mesh):
    in_specs = (
        P(("groups", "rep", "section"), "slide", None, None),
        P(),
        P(),
        P(),
        P(),
        P(None, "rep"),
        P("rep"),
        P("rep", None),
        P(),
        P(),
        P(),
        P(),
        P(("groups", "rep", "section"), "slide", None),
        P("slide", None),
        P(),
        P(None, "slide"),
        P(),
        P(("groups", "rep", "section"), None, None),
        P(("groups", "rep", "section")),
    )
    out_specs = (
        P(("groups", "rep", "section"), "slide", None),
        P(("groups", "rep", "section"), "slide", None),
    )
    return jax.shard_map(
        on_device, mesh=mesh, in_specs=in_specs, out_specs=out_specs, check_vma=False
    )
```

```python
import math

import jax
import jax.numpy as jnp
from jax import lax
from jax.experimental import pallas as pl
from jax.experimental.pallas import tpu as pltpu
from jax.sharding import PartitionSpec as P

SIDE = 7
KER = 7
HDIM = 64
LANES = 128


def layer_norm(inputs, gain, shift, epsilon):
    center = jnp.mean(inputs, axis=-1, keepdims=True)
    centered = inputs - center
    spread = jnp.mean(centered * centered, axis=-1, keepdims=True)
    return centered * lax.rsqrt(spread + epsilon) * gain + shift


def dw_ln_kernel(x_ref, w_ref, o_ref, conv_ref):
    C = x_ref.shape[-1]
    jrow = lax.broadcasted_iota(jnp.int32, (8, LANES), 0)
    masks = [((jrow + (bb - 3)) >= 0) & ((jrow + (bb - 3)) < SIDE) for bb in range(KER)]
    def chunk(ci, carry):
        c0 = pl.multiple_of(ci * LANES, LANES)
        rows = [x_ref[0, i, :, pl.ds(c0, LANES)].astype(jnp.float32) for i in range(SIDE)]
        bias = jnp.broadcast_to(w_ref[pl.ds(KER * KER, 1), pl.ds(c0, LANES)], (8, LANES))
        acc = [bias for _ in range(SIDE)]
        for ip in range(SIDE):
            for bb in range(KER):
                s = bb - 3
                sh = rows[ip] if s == 0 else pltpu.roll(rows[ip], shift=(-s) % 8, axis=0)
                sh = jnp.where(masks[bb], sh, 0.0)
                for a in range(KER):
                    i = ip - (a - 3)
                    if 0 <= i < SIDE:
                        wv = jnp.broadcast_to(w_ref[pl.ds(a * KER + bb, 1), pl.ds(c0, LANES)], (8, LANES))
                        acc[i] = acc[i] + sh * wv
        for i in range(SIDE):
            conv_ref[i, :, pl.ds(c0, LANES)] = acc[i]
        return carry
    lax.fori_loop(0, C // LANES, chunk, 0)
    g = w_ref[pl.ds(KER * KER + 1, 1), :]
    nb = w_ref[pl.ds(KER * KER + 2, 1), :]
    for i in range(SIDE):
        v = conv_ref[i]
        mean = jnp.mean(v, axis=-1, keepdims=True)
        cen = v - mean
        var = jnp.mean(cen * cen, axis=-1, keepdims=True)
        o_ref[0, i] = (cen * lax.rsqrt(var + 1e-06) * g + nb).astype(o_ref.dtype)

def dw_ln(tiles, depth_weight, depth_bias, norm_gain, norm_bias):
    T, _, C = tiles.shape
    x = jnp.pad(tiles.reshape(T, SIDE, SIDE, C), ((0, 0), (0, 0), (0, 1), (0, 0)))
    out = pl.pallas_call(
        dw_ln_kernel,
        grid=(T,),
        in_specs=[
            pl.BlockSpec((1, SIDE, 8, C), lambda t: (t, 0, 0, 0)),
            pl.BlockSpec((KER * KER + 3, C), lambda t: (0, 0)),
        ],
        out_specs=pl.BlockSpec((1, SIDE, 8, C), lambda t: (t, 0, 0, 0)),
        out_shape=jax.ShapeDtypeStruct((T, SIDE, 8, C), jnp.bfloat16),
        scratch_shapes=[pltpu.VMEM((SIDE, 8, C), jnp.float32)],
    )(x, jnp.concatenate([depth_weight, depth_bias[None], norm_gain[None], norm_bias[None]]))
    return out[:, :, :SIDE].reshape(T * SIDE * SIDE, C)


def normalize_heads(values):
    lead = values.shape[:-1]
    grouped = values.reshape(lead + (-1, 3, HDIM))
    paired = grouped[..., :2, :]
    scaled = paired * lax.rsqrt(jnp.mean(paired * paired, axis=-1, keepdims=True) + 1e-06)
    joined = jnp.concatenate([scaled, grouped[..., 2:, :]], axis=-2)
    return joined.astype(jnp.bfloat16).reshape(lead + (-1,))


def project(rows, partner_rows, cols, slide_gain):
    n_sec = lax.axis_size("section")
    both = jnp.dot(
        jnp.concatenate([rows, partner_rows], axis=0), cols, preferred_element_type=jnp.float32
    )
    count = rows.shape[0]
    mine = both[:count]
    from_partner = lax.ppermute(
        both[count:], "section", perm=[(c, (c + 1) % n_sec) for c in range(n_sec)]
    )
    projected = jnp.where(
        lax.axis_index("section") == 0,
        jnp.concatenate([mine, from_partner], axis=-1),
        jnp.concatenate([from_partner, mine], axis=-1),
    )
    return layer_norm(projected, slide_gain, 0.0, 1e-05).astype(jnp.bfloat16)


def on_device(
    tile_features,
    depth_weight,
    depth_bias,
    norm_gain,
    norm_bias,
    up_weight,
    up_bias,
    down_weight,
    down_bias,
    layer_scale,
    head_gain,
    head_bias,
    embed_store,
    in_weight,
    slide_gain,
    qkv_weight,
    head_slopes,
    tile_coords,
    valid_counts,
):
    n_sec = lax.axis_size("section")
    col_part = in_weight.shape[1] // n_sec
    my_cols = lax.dynamic_slice_in_dim(
        in_weight, lax.axis_index("section") * col_part, col_part, 1
    )
    cols_full = lax.all_gather(my_cols, "slide", axis=0, tiled=True)

    sec_swap = [(c, (c + 1) % n_sec) for c in range(n_sec)]
    fresh_count = tile_features.shape[1]
    partner_stored = lax.ppermute(embed_store[0, fresh_count:], "section", perm=sec_swap)

    tile_data = tile_features[0].astype(jnp.float32)
    fresh_count = tile_data.shape[0]
    n_rep = lax.axis_size("rep")
    my_rep = lax.axis_index("rep")
    n_slide = lax.axis_size("slide")
    my_slide = lax.axis_index("slide")
    normed = dw_ln(tile_features[0], depth_weight, depth_bias, norm_gain, norm_bias)

    def block_sums(rows):
        hidden = jax.nn.gelu(
            jnp.dot(rows, up_weight, preferred_element_type=jnp.float32) + up_bias,
            approximate=False,
        ).astype(jnp.bfloat16)
        part = jnp.dot(hidden, down_weight, preferred_element_type=jnp.float32).astype(
            jnp.bfloat16
        )
        tiles, per_tile = tile_data.shape[:2]
        owner = jnp.arange(tiles * per_tile, dtype=jnp.int32) // per_tile
        pool = (owner[None, :] == jnp.arange(tiles, dtype=jnp.int32)[:, None]).astype(
            jnp.bfloat16
        )
        return jnp.dot(pool, part, preferred_element_type=jnp.float32)

    received = [
        lax.ppermute(normed, "rep", perm=[(r, (r + k) % n_rep) for r in range(n_rep)])
        for k in range(1, n_rep)
    ]
    positions = tile_data.shape[1]
    own_term = jnp.mean(tile_data, axis=1) + layer_scale * (
        block_sums(normed) / positions + down_bias
    )
    peer_terms = [layer_scale * (block_sums(rows) / positions) for rows in received]
    returned = [
        lax.ppermute(term, "rep", perm=[(r, (r - k) % n_rep) for r in range(n_rep)])
        for k, term in enumerate(peer_terms, start=1)
    ]
    pooled = own_term
    for term in returned:
        pooled = pooled + term
    embedded = layer_norm(pooled, head_gain, head_bias, 1e-06).astype(jnp.bfloat16)
    partner_embedded = lax.ppermute(embedded, "section", perm=sec_swap)
    cols_full, embedded, partner_embedded = lax.optimization_barrier(
        (cols_full, embedded, partner_embedded)
    )

    seq_rows = jnp.concatenate([embedded, embed_store[0, fresh_count:]], axis=0)
    partner_rows = jnp.concatenate([partner_embedded, partner_stored], axis=0)
    normed_seq = project(seq_rows, partner_rows, cols_full, slide_gain)
    normed_all = lax.all_gather(normed_seq, "slide", axis=0, tiled=True)
    local_heads = normalize_heads(
        jnp.dot(normed_all, qkv_weight, preferred_element_type=jnp.float32)
    )
    seq_len = local_heads.shape[0]

    heads_here = local_heads.shape[1] // (3 * HDIM)
    arranged = local_heads.reshape(seq_len, heads_here, 3, HDIM)
    queries = arranged[:, :, 0]
    key_rows = arranged[:, :, 1]
    value_rows = arranged[:, :, 2]
    my_slopes = lax.dynamic_slice_in_dim(
        head_slopes, lax.axis_index("slide") * heads_here, heads_here, 0
    )
    coord_x = tile_coords[0, 0].astype(jnp.float32)
    coord_y = tile_coords[0, 1].astype(jnp.float32)
    valid = valid_counts[0]
    key_ok = jnp.arange(seq_len, dtype=jnp.int32) < valid
    inv_root = 1.0 / math.sqrt(HDIM)

    distance = jnp.abs(coord_x[:, None] - coord_x[None, :]) + jnp.abs(
        coord_y[:, None] - coord_y[None, :]
    )
    scores = (
        jnp.einsum("qhd,khd->hqk", queries, key_rows, preferred_element_type=jnp.float32)
        * inv_root
        - my_slopes[:, None, None] * distance[None]
    )
    weights = jnp.where(key_ok[None, None, :], jnp.exp(scores), 0.0).astype(jnp.bfloat16)
    totals = jnp.sum(weights, axis=-1, dtype=jnp.float32)
    weighted = jnp.einsum("hqk,khd->qhd", weights, value_rows, preferred_element_type=jnp.float32)
    safe = jnp.where(key_ok[None, :], totals, 1.0)
    attended = jnp.where(key_ok[:, None, None], weighted / safe.T[:, :, None], 0.0)
    attended = attended.astype(jnp.bfloat16).reshape(seq_len, heads_here * HDIM)
    context = lax.all_to_all(attended, "slide", split_axis=0, concat_axis=1, tiled=True)
    return (embedded[None], context[None])


def solution(mesh):
    in_specs = (
        P(("groups", "rep", "section"), "slide", None, None),
        P(),
        P(),
        P(),
        P(),
        P(None, "rep"),
        P("rep"),
        P("rep", None),
        P(),
        P(),
        P(),
        P(),
        P(("groups", "rep", "section"), "slide", None),
        P("slide", None),
        P(),
        P(None, "slide"),
        P(),
        P(("groups", "rep", "section"), None, None),
        P(("groups", "rep", "section")),
    )
    out_specs = (
        P(("groups", "rep", "section"), "slide", None),
        P(("groups", "rep", "section"), "slide", None),
    )
    return jax.shard_map(
        on_device, mesh=mesh, in_specs=in_specs, out_specs=out_specs, check_vma=False
    )
```

```python
import math

import jax
import jax.numpy as jnp
from jax import lax
from jax.experimental import pallas as pl
from jax.experimental.pallas import tpu as pltpu
from jax.sharding import PartitionSpec as P

SIDE = 7
KER = 7
HDIM = 64
LANES = 128


def layer_norm(inputs, gain, shift, epsilon):
    center = jnp.mean(inputs, axis=-1, keepdims=True)
    centered = inputs - center
    spread = jnp.mean(centered * centered, axis=-1, keepdims=True)
    return centered * lax.rsqrt(spread + epsilon) * gain + shift


def dw_ln_kernel(x_ref, w_ref, o_ref, conv_ref):
    C = x_ref.shape[-1]
    jrow = lax.broadcasted_iota(jnp.int32, (8, LANES), 0)
    masks = [((jrow + (bb - 3)) >= 0) & ((jrow + (bb - 3)) < SIDE) for bb in range(KER)]
    def chunk(ci, carry):
        c0 = pl.multiple_of(ci * LANES, LANES)
        rows = [x_ref[0, i, :, pl.ds(c0, LANES)].astype(jnp.float32) for i in range(SIDE)]
        bias = jnp.broadcast_to(w_ref[pl.ds(KER * KER, 1), pl.ds(c0, LANES)], (8, LANES))
        acc = [bias for _ in range(SIDE)]
        for ip in range(SIDE):
            for bb in range(KER):
                s = bb - 3
                sh = rows[ip] if s == 0 else pltpu.roll(rows[ip], shift=(-s) % 8, axis=0)
                sh = jnp.where(masks[bb], sh, 0.0)
                for a in range(KER):
                    i = ip - (a - 3)
                    if 0 <= i < SIDE:
                        wv = jnp.broadcast_to(w_ref[pl.ds(a * KER + bb, 1), pl.ds(c0, LANES)], (8, LANES))
                        acc[i] = acc[i] + sh * wv
        for i in range(SIDE):
            conv_ref[i, :, pl.ds(c0, LANES)] = acc[i]
        return carry
    lax.fori_loop(0, C // LANES, chunk, 0)
    g = w_ref[pl.ds(KER * KER + 1, 1), :]
    nb = w_ref[pl.ds(KER * KER + 2, 1), :]
    for i in range(SIDE):
        v = conv_ref[i]
        mean = jnp.mean(v, axis=-1, keepdims=True)
        cen = v - mean
        var = jnp.mean(cen * cen, axis=-1, keepdims=True)
        o_ref[0, i] = (cen * lax.rsqrt(var + 1e-06) * g + nb).astype(o_ref.dtype)

def dw_ln(tiles, depth_weight, depth_bias, norm_gain, norm_bias):
    T, _, C = tiles.shape
    x = jnp.pad(tiles.reshape(T, SIDE, SIDE, C), ((0, 0), (0, 0), (0, 1), (0, 0)))
    out = pl.pallas_call(
        dw_ln_kernel,
        grid=(T,),
        in_specs=[
            pl.BlockSpec((1, SIDE, 8, C), lambda t: (t, 0, 0, 0)),
            pl.BlockSpec((KER * KER + 3, C), lambda t: (0, 0)),
        ],
        out_specs=pl.BlockSpec((1, SIDE, 8, C), lambda t: (t, 0, 0, 0)),
        out_shape=jax.ShapeDtypeStruct((T, SIDE, 8, C), jnp.bfloat16),
        scratch_shapes=[pltpu.VMEM((SIDE, 8, C), jnp.float32)],
    )(x, jnp.concatenate([depth_weight, depth_bias[None], norm_gain[None], norm_bias[None]]))
    return out[:, :, :SIDE].reshape(T * SIDE * SIDE, C)


def normalize_heads(values):
    lead = values.shape[:-1]
    grouped = values.reshape(lead + (-1, 3, HDIM))
    paired = grouped[..., :2, :]
    scaled = paired * lax.rsqrt(jnp.mean(paired * paired, axis=-1, keepdims=True) + 1e-06)
    joined = jnp.concatenate([scaled, grouped[..., 2:, :]], axis=-2)
    return joined.astype(jnp.bfloat16).reshape(lead + (-1,))


def project(rows, partner_rows, cols, slide_gain):
    n_sec = lax.axis_size("section")
    both = jnp.dot(
        jnp.concatenate([rows, partner_rows], axis=0), cols, preferred_element_type=jnp.float32
    )
    count = rows.shape[0]
    mine = both[:count]
    from_partner = lax.ppermute(
        both[count:], "section", perm=[(c, (c + 1) % n_sec) for c in range(n_sec)]
    )
    projected = jnp.where(
        lax.axis_index("section") == 0,
        jnp.concatenate([mine, from_partner], axis=-1),
        jnp.concatenate([from_partner, mine], axis=-1),
    )
    return layer_norm(projected, slide_gain, 0.0, 1e-05).astype(jnp.bfloat16)


def on_device(
    tile_features,
    depth_weight,
    depth_bias,
    norm_gain,
    norm_bias,
    up_weight,
    up_bias,
    down_weight,
    down_bias,
    layer_scale,
    head_gain,
    head_bias,
    embed_store,
    in_weight,
    slide_gain,
    qkv_weight,
    head_slopes,
    tile_coords,
    valid_counts,
):
    n_sec = lax.axis_size("section")
    col_part = in_weight.shape[1] // n_sec
    my_cols = lax.dynamic_slice_in_dim(
        in_weight, lax.axis_index("section") * col_part, col_part, 1
    )
    cols_full = lax.all_gather(my_cols, "slide", axis=0, tiled=True)

    sec_swap = [(c, (c + 1) % n_sec) for c in range(n_sec)]
    fresh_count = tile_features.shape[1]

    tile_data = tile_features[0].astype(jnp.float32)
    fresh_count = tile_data.shape[0]
    n_rep = lax.axis_size("rep")
    my_rep = lax.axis_index("rep")
    n_slide = lax.axis_size("slide")
    my_slide = lax.axis_index("slide")
    normed = dw_ln(tile_features[0], depth_weight, depth_bias, norm_gain, norm_bias)

    def block_sums(rows):
        hidden = jax.nn.gelu(
            jnp.dot(rows, up_weight, preferred_element_type=jnp.float32) + up_bias,
            approximate=False,
        ).astype(jnp.bfloat16)
        part = jnp.dot(hidden, down_weight, preferred_element_type=jnp.float32).astype(
            jnp.bfloat16
        )
        return jnp.sum(part.astype(jnp.float32).reshape(tile_data.shape), axis=1)

    received = [
        lax.ppermute(normed, "rep", perm=[(r, (r + k) % n_rep) for r in range(n_rep)])
        for k in range(1, n_rep)
    ]
    positions = tile_data.shape[1]
    own_term = jnp.mean(tile_data, axis=1) + layer_scale * (
        block_sums(normed) / positions + down_bias
    )
    stored, own_term = lax.optimization_barrier((embed_store[0, fresh_count:], own_term))
    partner_stored = lax.ppermute(stored, "section", perm=sec_swap)
    peer_terms = [layer_scale * (block_sums(rows) / positions) for rows in received]
    returned = [
        lax.ppermute(term, "rep", perm=[(r, (r - k) % n_rep) for r in range(n_rep)])
        for k, term in enumerate(peer_terms, start=1)
    ]
    pooled = own_term
    for term in returned:
        pooled = pooled + term
    embedded = layer_norm(pooled, head_gain, head_bias, 1e-06).astype(jnp.bfloat16)
    partner_embedded = lax.ppermute(embedded, "section", perm=sec_swap)
    cols_full, embedded, partner_embedded = lax.optimization_barrier(
        (cols_full, embedded, partner_embedded)
    )

    seq_rows = jnp.concatenate([embedded, embed_store[0, fresh_count:]], axis=0)
    partner_rows = jnp.concatenate([partner_embedded, partner_stored], axis=0)
    normed_seq = project(seq_rows, partner_rows, cols_full, slide_gain)
    normed_all = lax.all_gather(normed_seq, "slide", axis=0, tiled=True)
    local_heads = normalize_heads(
        jnp.dot(normed_all, qkv_weight, preferred_element_type=jnp.float32)
    )
    seq_len = local_heads.shape[0]

    heads_here = local_heads.shape[1] // (3 * HDIM)
    arranged = local_heads.reshape(seq_len, heads_here, 3, HDIM)
    queries = arranged[:, :, 0]
    key_rows = arranged[:, :, 1]
    value_rows = arranged[:, :, 2]
    my_slopes = lax.dynamic_slice_in_dim(
        head_slopes, lax.axis_index("slide") * heads_here, heads_here, 0
    )
    coord_x = tile_coords[0, 0].astype(jnp.float32)
    coord_y = tile_coords[0, 1].astype(jnp.float32)
    valid = valid_counts[0]
    key_ok = jnp.arange(seq_len, dtype=jnp.int32) < valid
    inv_root = 1.0 / math.sqrt(HDIM)

    distance = jnp.abs(coord_x[:, None] - coord_x[None, :]) + jnp.abs(
        coord_y[:, None] - coord_y[None, :]
    )
    scores = (
        jnp.einsum("qhd,khd->hqk", queries, key_rows, preferred_element_type=jnp.float32)
        * inv_root
        - my_slopes[:, None, None] * distance[None]
    )
    weights = jnp.where(key_ok[None, None, :], jnp.exp(scores), 0.0).astype(jnp.bfloat16)
    totals = jnp.sum(weights, axis=-1, dtype=jnp.float32)
    weighted = jnp.einsum("hqk,khd->qhd", weights, value_rows, preferred_element_type=jnp.float32)
    safe = jnp.where(key_ok[None, :], totals, 1.0)
    attended = jnp.where(key_ok[:, None, None], weighted / safe.T[:, :, None], 0.0)
    attended = attended.astype(jnp.bfloat16).reshape(seq_len, heads_here * HDIM)
    context = lax.all_to_all(attended, "slide", split_axis=0, concat_axis=1, tiled=True)
    return (embedded[None], context[None])


def solution(mesh):
    in_specs = (
        P(("groups", "rep", "section"), "slide", None, None),
        P(),
        P(),
        P(),
        P(),
        P(None, "rep"),
        P("rep"),
        P("rep", None),
        P(),
        P(),
        P(),
        P(),
        P(("groups", "rep", "section"), "slide", None),
        P("slide", None),
        P(),
        P(None, "slide"),
        P(),
        P(("groups", "rep", "section"), None, None),
        P(("groups", "rep", "section")),
    )
    out_specs = (
        P(("groups", "rep", "section"), "slide", None),
        P(("groups", "rep", "section"), "slide", None),
    )
    return jax.shard_map(
        on_device, mesh=mesh, in_specs=in_specs, out_specs=out_specs, check_vma=False
    )
```

```python
import math

import jax
import jax.numpy as jnp
from jax import lax
from jax.experimental import pallas as pl
from jax.experimental.pallas import tpu as pltpu
from jax.sharding import PartitionSpec as P

SIDE = 7
KER = 7
HDIM = 64
LANES = 128


def layer_norm(inputs, gain, shift, epsilon):
    center = jnp.mean(inputs, axis=-1, keepdims=True)
    centered = inputs - center
    spread = jnp.mean(centered * centered, axis=-1, keepdims=True)
    return centered * lax.rsqrt(spread + epsilon) * gain + shift


def dw_ln_kernel(x_ref, w_ref, o_ref, conv_ref):
    C = x_ref.shape[-1]
    jrow = lax.broadcasted_iota(jnp.int32, (8, LANES), 0)
    masks = [((jrow + (bb - 3)) >= 0) & ((jrow + (bb - 3)) < SIDE) for bb in range(KER)]
    def chunk(ci, carry):
        c0 = pl.multiple_of(ci * LANES, LANES)
        rows = [x_ref[0, i, :, pl.ds(c0, LANES)].astype(jnp.float32) for i in range(SIDE)]
        bias = jnp.broadcast_to(w_ref[pl.ds(KER * KER, 1), pl.ds(c0, LANES)], (8, LANES))
        acc = [bias for _ in range(SIDE)]
        for ip in range(SIDE):
            for bb in range(KER):
                s = bb - 3
                sh = rows[ip] if s == 0 else pltpu.roll(rows[ip], shift=(-s) % 8, axis=0)
                sh = jnp.where(masks[bb], sh, 0.0)
                for a in range(KER):
                    i = ip - (a - 3)
                    if 0 <= i < SIDE:
                        wv = jnp.broadcast_to(w_ref[pl.ds(a * KER + bb, 1), pl.ds(c0, LANES)], (8, LANES))
                        acc[i] = acc[i] + sh * wv
        for i in range(SIDE):
            conv_ref[i, :, pl.ds(c0, LANES)] = acc[i]
        return carry
    lax.fori_loop(0, C // LANES, chunk, 0)
    g = w_ref[pl.ds(KER * KER + 1, 1), :]
    nb = w_ref[pl.ds(KER * KER + 2, 1), :]
    for i in range(SIDE):
        v = conv_ref[i]
        mean = jnp.mean(v, axis=-1, keepdims=True)
        cen = v - mean
        var = jnp.mean(cen * cen, axis=-1, keepdims=True)
        o_ref[0, i] = (cen * lax.rsqrt(var + 1e-06) * g + nb).astype(o_ref.dtype)

def dw_ln(tiles, depth_weight, depth_bias, norm_gain, norm_bias):
    T, _, C = tiles.shape
    x = jnp.pad(tiles.reshape(T, SIDE, SIDE, C), ((0, 0), (0, 0), (0, 1), (0, 0)))
    out = pl.pallas_call(
        dw_ln_kernel,
        grid=(T,),
        in_specs=[
            pl.BlockSpec((1, SIDE, 8, C), lambda t: (t, 0, 0, 0)),
            pl.BlockSpec((KER * KER + 3, C), lambda t: (0, 0)),
        ],
        out_specs=pl.BlockSpec((1, SIDE, 8, C), lambda t: (t, 0, 0, 0)),
        out_shape=jax.ShapeDtypeStruct((T, SIDE, 8, C), jnp.bfloat16),
        scratch_shapes=[pltpu.VMEM((SIDE, 8, C), jnp.float32)],
    )(x, jnp.concatenate([depth_weight, depth_bias[None], norm_gain[None], norm_bias[None]]))
    return out[:, :, :SIDE].reshape(T * SIDE * SIDE, C)


def normalize_heads(values):
    lead = values.shape[:-1]
    grouped = values.reshape(lead + (-1, 3, HDIM))
    paired = grouped[..., :2, :]
    scaled = paired * lax.rsqrt(jnp.mean(paired * paired, axis=-1, keepdims=True) + 1e-06)
    joined = jnp.concatenate([scaled, grouped[..., 2:, :]], axis=-2)
    return joined.astype(jnp.bfloat16).reshape(lead + (-1,))


def project(rows, partner_rows, cols, slide_gain):
    n_sec = lax.axis_size("section")
    for_partner = jnp.dot(partner_rows, cols, preferred_element_type=jnp.float32)
    from_partner = lax.ppermute(
        for_partner, "section", perm=[(c, (c + 1) % n_sec) for c in range(n_sec)]
    )
    mine = jnp.dot(rows, cols, preferred_element_type=jnp.float32)
    projected = jnp.where(
        lax.axis_index("section") == 0,
        jnp.concatenate([mine, from_partner], axis=-1),
        jnp.concatenate([from_partner, mine], axis=-1),
    )
    return layer_norm(projected, slide_gain, 0.0, 1e-05).astype(jnp.bfloat16)


def on_device(
    tile_features,
    depth_weight,
    depth_bias,
    norm_gain,
    norm_bias,
    up_weight,
    up_bias,
    down_weight,
    down_bias,
    layer_scale,
    head_gain,
    head_bias,
    embed_store,
    in_weight,
    slide_gain,
    qkv_weight,
    head_slopes,
    tile_coords,
    valid_counts,
):
    n_sec = lax.axis_size("section")
    col_part = in_weight.shape[1] // n_sec
    my_cols = lax.dynamic_slice_in_dim(
        in_weight, lax.axis_index("section") * col_part, col_part, 1
    )
    cols_full = lax.all_gather(my_cols, "slide", axis=0, tiled=True)

    sec_swap = [(c, (c + 1) % n_sec) for c in range(n_sec)]
    fresh_count = tile_features.shape[1]

    tile_data = tile_features[0].astype(jnp.float32)
    fresh_count = tile_data.shape[0]
    n_rep = lax.axis_size("rep")
    my_rep = lax.axis_index("rep")
    n_slide = lax.axis_size("slide")
    my_slide = lax.axis_index("slide")
    normed = dw_ln(tile_features[0], depth_weight, depth_bias, norm_gain, norm_bias)

    def block_sums(rows):
        hidden = jax.nn.gelu(
            jnp.dot(rows, up_weight, preferred_element_type=jnp.float32) + up_bias,
            approximate=False,
        ).astype(jnp.bfloat16)
        part = jnp.dot(hidden, down_weight, preferred_element_type=jnp.float32).astype(
            jnp.bfloat16
        )
        return jnp.sum(part.astype(jnp.float32).reshape(tile_data.shape), axis=1)

    received = [
        lax.ppermute(normed, "rep", perm=[(r, (r + k) % n_rep) for r in range(n_rep)])
        for k in range(1, n_rep)
    ]
    positions = tile_data.shape[1]
    own_term = jnp.mean(tile_data, axis=1) + layer_scale * (
        block_sums(normed) / positions + down_bias
    )
    stored, own_term = lax.optimization_barrier((embed_store[0, fresh_count:], own_term))
    partner_stored = lax.ppermute(stored, "section", perm=sec_swap)
    peer_terms = [layer_scale * (block_sums(rows) / positions) for rows in received]
    returned = [
        lax.ppermute(term, "rep", perm=[(r, (r - k) % n_rep) for r in range(n_rep)])
        for k, term in enumerate(peer_terms, start=1)
    ]
    pooled = own_term
    for term in returned:
        pooled = pooled + term
    embedded = layer_norm(pooled, head_gain, head_bias, 1e-06).astype(jnp.bfloat16)
    partner_embedded = lax.ppermute(embedded, "section", perm=sec_swap)
    cols_full, embedded, partner_embedded = lax.optimization_barrier(
        (cols_full, embedded, partner_embedded)
    )

    seq_rows = jnp.concatenate([embedded, embed_store[0, fresh_count:]], axis=0)
    partner_rows = jnp.concatenate([partner_embedded, partner_stored], axis=0)
    normed_seq = project(seq_rows, partner_rows, cols_full, slide_gain)
    normed_all = lax.all_gather(normed_seq, "slide", axis=0, tiled=True)
    local_heads = normalize_heads(
        jnp.dot(normed_all, qkv_weight, preferred_element_type=jnp.float32)
    )
    seq_len = local_heads.shape[0]

    heads_here = local_heads.shape[1] // (3 * HDIM)
    arranged = local_heads.reshape(seq_len, heads_here, 3, HDIM)
    queries = arranged[:, :, 0]
    key_rows = arranged[:, :, 1]
    value_rows = arranged[:, :, 2]
    my_slopes = lax.dynamic_slice_in_dim(
        head_slopes, lax.axis_index("slide") * heads_here, heads_here, 0
    )
    coord_x = tile_coords[0, 0].astype(jnp.float32)
    coord_y = tile_coords[0, 1].astype(jnp.float32)
    valid = valid_counts[0]
    key_ok = jnp.arange(seq_len, dtype=jnp.int32) < valid
    inv_root = 1.0 / math.sqrt(HDIM)

    distance = jnp.abs(coord_x[:, None] - coord_x[None, :]) + jnp.abs(
        coord_y[:, None] - coord_y[None, :]
    )
    scores = (
        jnp.einsum("qhd,khd->hqk", queries, key_rows, preferred_element_type=jnp.float32)
        * inv_root
        - my_slopes[:, None, None] * distance[None]
    )
    weights = jnp.where(key_ok[None, None, :], jnp.exp(scores), 0.0).astype(jnp.bfloat16)
    totals = jnp.sum(weights, axis=-1, dtype=jnp.float32)
    weighted = jnp.einsum("hqk,khd->qhd", weights, value_rows, preferred_element_type=jnp.float32)
    safe = jnp.where(key_ok[None, :], totals, 1.0)
    attended = jnp.where(key_ok[:, None, None], weighted / safe.T[:, :, None], 0.0)
    attended = attended.astype(jnp.bfloat16).reshape(seq_len, heads_here * HDIM)
    context = lax.all_to_all(attended, "slide", split_axis=0, concat_axis=1, tiled=True)
    return (embedded[None], context[None])


def solution(mesh):
    in_specs = (
        P(("groups", "rep", "section"), "slide", None, None),
        P(),
        P(),
        P(),
        P(),
        P(None, "rep"),
        P("rep"),
        P("rep", None),
        P(),
        P(),
        P(),
        P(),
        P(("groups", "rep", "section"), "slide", None),
        P("slide", None),
        P(),
        P(None, "slide"),
        P(),
        P(("groups", "rep", "section"), None, None),
        P(("groups", "rep", "section")),
    )
    out_specs = (
        P(("groups", "rep", "section"), "slide", None),
        P(("groups", "rep", "section"), "slide", None),
    )
    return jax.shard_map(
        on_device, mesh=mesh, in_specs=in_specs, out_specs=out_specs, check_vma=False
    )
```
